32 devices in a mesh: runs: 2 (over x), tile: 16 (over z, y, core).
Axes of the slice: x: 2, y: 2, z: 4, core: 2. Of those that a mesh axis runs over, the one named last changes fastest.
Arguments:
- fluid_press: float32 [8192, 128], P(('runs', 'tile')), parts along dimension 0, may hold values from -6 to 6
- iterate: float32 [8192, 128], P(('runs', 'tile')), parts along dimension 0, may hold values from -6 to 6
- displace: float32 [4096, 128], P(('runs', 'tile')), parts along dimension 0, may hold values from -6 to 6
- velocity: float32 [4096, 128], P(('runs', 'tile')), parts along dimension 0, may hold values from -6 to 6
- stiffness: float32 [4096, 128], P(('runs', 'tile')), parts along dimension 0, may hold values from 0.08 to 0.45
- owners: int32 [4096, 1], P(('runs', 'tile')), parts along dimension 0, may hold values from 0 to 15; in each aligned block of 128 rows (0 to 127, 128 to 255, ...) at most 16 rows name the same one
- diff_cur: bfloat16 [40, 8192, 128], P(None, ('runs', 'tile')), parts along dimension 1, may hold values from -1.1048543 to 1.1048543
- step_cur: bfloat16 [40, 8192, 128], P(None, ('runs', 'tile')), parts along dimension 1, may hold values from -6 to 6
- diff_past: bfloat16 [30, 8192, 128], P(None, ('runs', 'tile')), parts along dimension 1, may hold values from -1.1048543 to 1.1048543
- step_past: bfloat16 [30, 8192, 128], P(None, ('runs', 'tile')), parts along dimension 1, may hold values from -6 to 6
Outputs:
- new_iterate: float32 [8192, 128], P(('runs', 'tile')), parts along dimension 0
- displace_out: float32 [4096, 128], P(('runs', 'tile')), parts along dimension 0
- velocity_out: float32 [4096, 128], P(('runs', 'tile')), parts along dimension 0
The draws below stay inside these ranges and needn't reach their ends.
There are 2 independent parts, one for each index of `runs`. The reference program is written for one: setup_inputs(seed, part) draws one part's arguments, and reference() takes and returns one part's arrays. A program takes and returns all parts, laid end to end along the dimension named above; each array names one. Nothing has to cross between parts.
Inputs may be any that keep to these rules, and one draw needn't show every extreme that they name: `owners`: in the 128 lines of one device no partition is named more than 16 times; some partition is named exactly 16 times.
All inputs are finite; a program needn't handle non-finite values.
Results may differ from the reference program's by a relative error of at most 0.0042.
Values sent between devices are 32-bit elements; how exact they have to be, the bound alone decides.
No kernel may reach another device: no remote copies, remote signals or barrier semaphores. Data moves between devices by JAX's collectives and lax.ppermute only.
A program may use at most 64 MiB of HBM per device.

```python
import math
import jax
import jax.numpy as jnp
import numpy as np
from jax import lax

LINE = 128
BLK_DEV = 128
CUR = 40
PAST = 30
SUBSTEPS = 4
MOST = 16
SLOTS_DEV = 256
BLOCKS = 2048
FLUID_ROWS = 4096
N_TILE = 16


def shared_parts(key):
    common = jax.random.truncated_normal(jax.random.fold_in(key, 7), -4.0, 4.0, (FLUID_ROWS, LINE))
    weight = 0.5
    return (common, weight)


def history(key, marker, count):
    common, weight = shared_parts(key)
    own_part = jax.random.truncated_normal(jax.random.fold_in(key, marker), -4.0, 4.0, (count, FLUID_ROWS, LINE))
    col_scale = jnp.exp(jax.random.uniform(jax.random.fold_in(key, marker + 1), (count, 1, 1), minval=0.0, maxval=math.log(10.0)))
    norm = (FLUID_ROWS * LINE) ** (-0.5)
    values = (own_part + weight * common[None]) * col_scale * norm
    return values.astype(jnp.bfloat16)


def draw_diff_cur(key, part):
    return history(key, 11, CUR)


def draw_diff_past(key, part):
    return history(key, 21, PAST)


def level_of(own_key, shape, split, low, top_value):
    def one(position, parts):
        steps = jax.random.uniform(jax.random.fold_in(jax.random.fold_in(own_key, 6), position), (parts,), jnp.float32, low / len(split), top_value / len(split))
        return jnp.repeat(jnp.exp(steps), shape[position] // parts).reshape((-1,) + (1,) * (len(shape) - position - 1))

    level = one(*split[0])
    for cut in split[1:]:
        level = level * one(*cut)
    return level


def assign_block(stream_key, own, number, rows, number_of, top, reach, lean):
    order = jax.random.permutation(stream_key, number_of)
    heavy_load, usual = load_shares(number_of, rows * top, reach, lean, True), load_shares(number_of, rows * top, reach, lean, False)
    places = jnp.arange(number_of)

    def named(sizes, offset_by):
        used = int((sizes > 0).sum())
        fixed = max(1, used // 4)
        passed = fixed + (places - fixed + offset_by * (used - fixed)) % max(1, number_of - fixed)
        return jnp.zeros((number_of,), jnp.int32).at[order[jnp.where(places < fixed, places, passed)]].set(jnp.asarray(sizes, jnp.int32))

    sizes = jnp.where(number % 4 == 0, named(heavy_load, number // 4), named(usual, number - number // 4 - 1))
    mixed = jax.random.permutation(jax.random.fold_in(own, 3), number_of)
    donor, sink = mixed[0:number_of // 2 * 2:2], mixed[1:number_of // 2 * 2:2]
    slack = jnp.minimum(sizes[donor] - 1, reach - sizes[sink]) // 2
    slack = jnp.where((donor == order[0]) | (sink == order[0]) | (sizes[sink] == 0), 0, jnp.maximum(slack, 0))
    passed = jax.random.randint(jax.random.fold_in(own, 4), (number_of // 2,), 0, 1 << 20) % (slack + 1)
    sizes = sizes.at[donor].add(-passed).at[sink].add(passed)
    labels = jnp.searchsorted(jnp.cumsum(sizes), jnp.arange(rows * top), side="right").astype(jnp.int32)
    listing = labels.reshape(top, rows).T
    listing = listing[jax.random.permutation(jax.random.fold_in(own, 1), rows)]
    offset_by = jax.random.randint(jax.random.fold_in(own, 2), (rows, 1), 0, top)
    return jnp.take_along_axis(listing, (jnp.arange(top)[None, :] + offset_by) % top, axis=1)


def load_shares(amount, total, bound, skew, full):
    weights = [(1 << 20) // math.isqrt(standing ** skew) + 1 for standing in range(1, amount + 1)]
    largest = bound if full else min(bound, max(-(-total // amount), total * weights[0] // sum(weights)))
    least = 1 if total - largest >= amount - 1 else 0
    holding, spare = [largest] + [least] * (amount - 1), total - largest - least * (amount - 1)
    while spare > 0:
        free = [i for i in range(1, amount) if holding[i] < largest] or [i for i in range(1, amount) if holding[i] < bound]
        whole, left = sum([weights[i] for i in free]), spare
        for i in free:
            extra = min(bound - holding[i], max(1, left * weights[i] // whole), spare)
            holding[i] = holding[i] + extra
            spare = spare - extra
    return np.array(holding)


def normal_values(stream_key, extent, spread, reach, shards=(), kind=jnp.bfloat16):
    drawn = spread * jax.random.normal(stream_key, extent, jnp.float32)
    if shards:
        drawn = drawn * level_of(stream_key, extent, shards, -0.22, 0.18)
    return jnp.clip(drawn, -reach, reach).astype(kind)


def setup_inputs(seed: int = 0, part: int = 0) -> dict:
    seeds = jax.random.split(jax.random.key(seed), 11)
    part_keys = jax.random.split(jax.random.fold_in(seeds[10], part), 11)
    fluid_press = normal_values(part_keys[0], (FLUID_ROWS, LINE), 1.0, 6.0, ((0, 16),), jnp.float32)
    iterate = normal_values(part_keys[1], (FLUID_ROWS, LINE), 1.0, 6.0, ((0, 16),), jnp.float32)
    displace = normal_values(part_keys[2], (BLOCKS, LINE), 1.0, 6.0, ((0, 16),), jnp.float32)
    velocity = normal_values(part_keys[3], (BLOCKS, LINE), 0.5, 6.0, ((0, 16),), jnp.float32)
    stiffness = jnp.clip(jnp.exp(math.log(0.45) - 1.7272209 * jax.random.uniform(part_keys[4], (BLOCKS, LINE), jnp.float32) ** level_of(part_keys[4], (BLOCKS, LINE), ((0, 16),), -0.2, 0.2)), 0.08, 0.45)
    owners_keys = jax.random.split(jax.random.fold_in(part_keys[5], 1), BLOCKS // BLK_DEV)
    owners_turns = jax.random.permutation(jax.random.fold_in(part_keys[5], 3), BLOCKS // BLK_DEV)
    owners = jax.vmap(lambda own, number: assign_block(jax.random.fold_in(part_keys[5], 2), own, number, BLK_DEV, N_TILE, 1, MOST, 2))(owners_keys, owners_turns).reshape((BLOCKS, 1))
    diff_cur = draw_diff_cur(jax.random.fold_in(jax.random.fold_in(seeds[10], part), 71), part)
    step_cur = normal_values(part_keys[7], (CUR, FLUID_ROWS, LINE), 1.0, 6.0, ((1, 16),))
    diff_past = draw_diff_past(jax.random.fold_in(jax.random.fold_in(seeds[10], part), 71), part)
    step_past = normal_values(part_keys[9], (PAST, FLUID_ROWS, LINE), 1.0, 6.0, ((1, 16),))
    return {"fluid_press": fluid_press, "iterate": iterate, "displace": displace, "velocity": velocity, "stiffness": stiffness, "owners": owners, "diff_cur": diff_cur, "step_cur": step_cur, "diff_past": diff_past, "step_past": step_past}


step_dt = 1.0
damping = 0.05

def march(field, speed, stiffness, pressure):
    for substep in range(SUBSTEPS):
        upper = jnp.roll(field, 1, 0)
        beneath = jnp.roll(field, -1, 0)
        zero_col = jnp.zeros((field.shape[0], 1), jnp.float32)
        left = jnp.concatenate([zero_col, field[:, :-1]], 1)
        right = jnp.concatenate([field[:, 1:], zero_col], 1)
        lapl = upper + beneath + (left + right) - 4.0 * field
        speed = speed + step_dt * (stiffness * lapl + pressure - damping * speed)
        field = field + step_dt * speed
    return (field, speed)

def solve_spd(matrix, vector):
    factor = jnp.linalg.cholesky(matrix)
    inner = lax.linalg.triangular_solve(factor, vector[:, None], left_side=True, lower=True)
    outer = lax.linalg.triangular_solve(factor, inner, left_side=True, lower=True, transpose_a=True)
    return outer[:, 0]

def reference(fluid_press, iterate, displace, velocity, stiffness, owners, diff_cur, step_cur, diff_past, step_past):
    high = lax.Precision.HIGHEST
    table = owners[:, 0].reshape(N_TILE, BLK_DEV)
    onehot = (table[:, :, None] == jnp.arange(N_TILE, dtype=jnp.int32)[None, None, :]).astype(jnp.float32)
    below = (jnp.arange(BLK_DEV)[:, None] > jnp.arange(BLK_DEV)[None, :]).astype(jnp.float32)
    earlier = jnp.einsum('ij,sjn->sin', below, onehot, precision=high)
    rank_in = jnp.sum(earlier * onehot, axis=2).astype(jnp.int32)
    sources = jnp.arange(N_TILE, dtype=jnp.int32)[:, None]
    slots = (table * SLOTS_DEV + sources * MOST + rank_in).reshape(-1).astype(jnp.int32)
    mask = jnp.zeros((FLUID_ROWS,), jnp.float32).at[slots].set(1.0)
    pressure = fluid_press[slots]
    field, speed = march(displace, velocity, stiffness, pressure)
    x_tilde = jnp.zeros((FLUID_ROWS, LINE), jnp.float32).at[slots].set(field)
    resid = (mask[:, None] * (x_tilde - iterate)).astype(jnp.bfloat16)
    resid_flat = resid.astype(jnp.float32).reshape(-1)
    cur_cols = (diff_cur.astype(jnp.float32) * mask[None, :, None]).reshape(CUR, -1)
    past_cols = (diff_past.astype(jnp.float32) * mask[None, :, None]).reshape(PAST, -1)
    gram_cur = jnp.dot(cur_cols, cur_cols.T, precision=high)
    rhs_cur = jnp.dot(cur_cols, resid_flat, precision=high)
    gram_past = jnp.dot(past_cols, past_cols.T, precision=high)
    coeff = -solve_spd(gram_cur, rhs_cur)
    proj = resid_flat + jnp.dot(coeff, cur_cols, precision=high)
    past = solve_spd(gram_past, jnp.dot(past_cols, proj, precision=high))
    coeff_half = coeff.astype(jnp.bfloat16).astype(jnp.float32)
    past_half = past.astype(jnp.bfloat16).astype(jnp.float32)
    upd_cur = jnp.dot(coeff_half, step_cur.astype(jnp.float32).reshape(CUR, -1), precision=high)
    upd_past = jnp.dot(past_half, step_past.astype(jnp.float32).reshape(PAST, -1), precision=high)
    update = (upd_cur - upd_past).reshape(FLUID_ROWS, LINE)
    new_iterate = mask[:, None] * (x_tilde + update)
    return (new_iterate, field, speed)
```

```python
import jax
import jax.numpy as jnp
from jax import lax
from jax.sharding import PartitionSpec as P

SUBSTEPS = 4


step_dt = 1.0
damping = 0.05


def tree_sum(value, axis):
    count = lax.axis_size(axis)
    if count & (count - 1):
        return lax.psum(value, axis)
    stride = 1
    while stride < count:
        value = value + lax.ppermute(value, axis, [(i, i ^ stride) for i in range(count)])
        stride *= 2
    return value


def with_halo(cells, width, axis):
    count = lax.axis_size(axis)
    below = lax.ppermute(cells[-width:], axis, [(i, (i + 1) % count) for i in range(count)])
    above = lax.ppermute(cells[:width], axis, [((i + 1) % count, i) for i in range(count)])
    return jnp.concatenate([below, cells, above], axis=0)


def sides(center):
    zero_col = jnp.zeros((center.shape[0], 1), jnp.float32)
    left = jnp.concatenate([zero_col, center[:, :-1]], 1)
    right = jnp.concatenate([center[:, 1:], zero_col], 1)
    return left + right


def solve_spd(factor, vector):
    inner = lax.linalg.triangular_solve(factor, vector[:, None], left_side=True, lower=True)
    outer = lax.linalg.triangular_solve(factor, inner, left_side=True, lower=True, transpose_a=True)
    return outer[:, 0]


def local(
    fluid_press,
    iterate,
    displace,
    velocity,
    stiffness,
    owners,
    diff_cur,
    step_cur,
    diff_past,
    step_past,
):
    high = lax.Precision.HIGHEST
    tile_count = lax.axis_size("tile")
    line_count = displace.shape[0]
    slot_count = iterate.shape[0]
    per_pair = slot_count // tile_count
    n_cur = diff_cur.shape[0]
    owner_list = owners[:, 0]
    onehot = (owner_list[:, None] == jnp.arange(tile_count, dtype=jnp.int32)[None, :]).astype(
        jnp.float32
    )
    below = (jnp.arange(line_count)[:, None] > jnp.arange(line_count)[None, :]).astype(jnp.float32)
    earlier = jnp.dot(below, onehot, precision=high)
    rank_in = jnp.sum(earlier * onehot, axis=1).astype(jnp.int32)
    slot_of = owner_list * per_pair + rank_in
    chooser = (slot_of[:, None] == jnp.arange(slot_count, dtype=jnp.int32)[None, :]).astype(
        jnp.float32
    )
    flags = jnp.sum(chooser, axis=0)
    mask = lax.all_to_all(flags, "tile", split_axis=0, concat_axis=0, tiled=True)
    mask_half = mask.astype(jnp.bfloat16)

    cols = jnp.concatenate(
        [
            (diff_cur * mask_half[None, :, None]).reshape(n_cur, -1),
            (diff_past * mask_half[None, :, None]).reshape(diff_past.shape[0], -1),
        ],
        axis=0,
    )
    gram = lax.dot_general(cols, cols, (((1,), (1,)), ((), ())), preferred_element_type=jnp.float32)
    gram = tree_sum(gram, "tile")
    gram_cur = gram[:n_cur, :n_cur]
    gram_past = gram[n_cur:, n_cur:]
    cross = gram[n_cur:, :n_cur]
    factor_cur = jnp.linalg.cholesky(gram_cur)
    factor_past = jnp.linalg.cholesky(gram_past)

    returned = lax.all_to_all(fluid_press, "tile", split_axis=0, concat_axis=0, tiled=True)
    pressure = jnp.dot(chooser, returned, precision=high)

    width = SUBSTEPS
    packed = with_halo(jnp.concatenate([displace, velocity, stiffness, pressure], axis=1), width, "tile")
    lanes = displace.shape[1]
    field = packed[:, :lanes]
    speed = packed[:, lanes : 2 * lanes]
    stiff = packed[:, 2 * lanes : 3 * lanes]
    press = packed[:, 3 * lanes :]
    for substep in range(SUBSTEPS):
        lapl = jnp.roll(field, 1, 0) + jnp.roll(field, -1, 0) + sides(field) - 4.0 * field
        speed = speed + step_dt * (stiff * lapl + press - damping * speed)
        field = field + step_dt * speed
    field = field[width : width + line_count]
    speed = speed[width : width + line_count]

    outgoing = jnp.dot(chooser.T, field, precision=high)
    x_tilde = lax.all_to_all(outgoing, "tile", split_axis=0, concat_axis=0, tiled=True)
    resid = (mask[:, None] * (x_tilde - iterate)).astype(jnp.bfloat16).reshape(-1)
    inner = tree_sum(jnp.dot(cols, resid, preferred_element_type=jnp.float32), "tile")
    rhs_cur = inner[:n_cur]
    rhs_past = inner[n_cur:]
    coeff = -solve_spd(factor_cur, rhs_cur)
    projected = rhs_past + jnp.dot(cross, coeff, precision=high)
    past = solve_spd(factor_past, projected)
    upd_cur = jnp.dot(
        coeff.astype(jnp.bfloat16),
        step_cur.reshape(step_cur.shape[0], -1),
        preferred_element_type=jnp.float32,
    )
    upd_past = jnp.dot(
        past.astype(jnp.bfloat16),
        step_past.reshape(step_past.shape[0], -1),
        preferred_element_type=jnp.float32,
    )
    update = (upd_cur - upd_past).reshape(x_tilde.shape)
    new_iterate = mask[:, None] * (x_tilde + update)
    return (new_iterate, field, speed)


def solution(mesh):
    placed = (
        P(("runs", "tile"), None),
        P(("runs", "tile"), None),
        P(("runs", "tile"), None),
        P(("runs", "tile"), None),
        P(("runs", "tile"), None),
        P(("runs", "tile"), None),
        P(None, ("runs", "tile"), None),
        P(None, ("runs", "tile"), None),
        P(None, ("runs", "tile"), None),
        P(None, ("runs", "tile"), None),
    )
    return jax.shard_map(
        local,
        mesh=mesh,
        in_specs=placed,
        out_specs=(P(("runs", "tile"), None), P(("runs", "tile"), None), P(("runs", "tile"), None)),
        check_vma=False,
    )
```

```python
import jax
import jax.numpy as jnp
from jax import lax
from jax.sharding import PartitionSpec as P

SUBSTEPS = 4


step_dt = 1.0
damping = 0.05


def tree_sum(value, axis):
    count = lax.axis_size(axis)
    if count & (count - 1):
        return lax.psum(value, axis)
    stride = 1
    while stride < count:
        value = value + lax.ppermute(value, axis, [(i, i ^ stride) for i in range(count)])
        stride *= 2
    return value


def halo_pair(cells, width, axis):
    count = lax.axis_size(axis)
    below = lax.ppermute(cells[-width:], axis, [(i, (i + 1) % count) for i in range(count)])
    above = lax.ppermute(cells[:width], axis, [((i + 1) % count, i) for i in range(count)])
    return below, above


def sides(center):
    zero_col = jnp.zeros((center.shape[0], 1), jnp.float32)
    left = jnp.concatenate([zero_col, center[:, :-1]], 1)
    right = jnp.concatenate([center[:, 1:], zero_col], 1)
    return left + right


def inverse_factor(matrix):
    factor = jnp.linalg.cholesky(matrix)
    eye = jnp.eye(matrix.shape[0], dtype=matrix.dtype)
    return lax.linalg.triangular_solve(factor, eye, left_side=True, lower=True)


def solve_spd(inverse, vector):
    high = lax.Precision.HIGHEST
    inner = jnp.dot(inverse, vector, precision=high)
    return jnp.dot(inverse.T, inner, precision=high)


def local(
    fluid_press,
    iterate,
    displace,
    velocity,
    stiffness,
    owners,
    diff_cur,
    step_cur,
    diff_past,
    step_past,
):
    high = lax.Precision.HIGHEST
    tile_count = lax.axis_size("tile")
    line_count = displace.shape[0]
    slot_count = iterate.shape[0]
    per_pair = slot_count // tile_count
    n_cur = diff_cur.shape[0]
    owner_list = owners[:, 0]
    onehot = (owner_list[:, None] == jnp.arange(tile_count, dtype=jnp.int32)[None, :]).astype(
        jnp.float32
    )
    below = (jnp.arange(line_count)[:, None] > jnp.arange(line_count)[None, :]).astype(jnp.float32)
    earlier = jnp.dot(below, onehot, precision=high)
    rank_in = jnp.sum(earlier * onehot, axis=1).astype(jnp.int32)
    slot_of = owner_list * per_pair + rank_in
    chooser = (slot_of[:, None] == jnp.arange(slot_count, dtype=jnp.int32)[None, :]).astype(
        jnp.float32
    )
    flags = jnp.sum(chooser, axis=0)
    lanes = fluid_press.shape[1]
    width = SUBSTEPS

    edge = jnp.concatenate([displace, velocity, stiffness], axis=1)
    edge_below, edge_above = halo_pair(edge, width, "tile")

    flag_rows = jnp.zeros((tile_count, 1, lanes), jnp.float32)
    flag_rows = flag_rows.at[:, 0, :per_pair].set(flags.reshape(tile_count, per_pair))
    sent = jnp.concatenate([fluid_press.reshape(tile_count, per_pair, lanes), flag_rows], axis=1)
    got = lax.all_to_all(sent, "tile", split_axis=0, concat_axis=0, tiled=True)
    returned = got[:, :per_pair, :].reshape(slot_count, lanes)
    mask = got[:, per_pair, :per_pair].reshape(slot_count)
    mask_half = mask.astype(jnp.bfloat16)

    cols = jnp.concatenate(
        [
            (diff_cur * mask_half[None, :, None]).reshape(n_cur, -1),
            (diff_past * mask_half[None, :, None]).reshape(diff_past.shape[0], -1),
        ],
        axis=0,
    )
    gram = lax.dot_general(cols, cols, (((1,), (1,)), ((), ())), preferred_element_type=jnp.float32)
    gram = tree_sum(gram, "tile")
    cross = gram[n_cur:, :n_cur]
    inv_cur = inverse_factor(gram[:n_cur, :n_cur])
    inv_past = inverse_factor(gram[n_cur:, n_cur:])

    pressure = jnp.dot(chooser, returned, precision=high)
    press_below, press_above = halo_pair(pressure, width, "tile")
    packed = jnp.concatenate(
        [
            jnp.concatenate([edge_below, press_below], axis=1),
            jnp.concatenate([edge, pressure], axis=1),
            jnp.concatenate([edge_above, press_above], axis=1),
        ],
        axis=0,
    )
    field = packed[:, :lanes]
    speed = packed[:, lanes : 2 * lanes]
    stiff = packed[:, 2 * lanes : 3 * lanes]
    press = packed[:, 3 * lanes :]
    for substep in range(SUBSTEPS):
        lapl = jnp.roll(field, 1, 0) + jnp.roll(field, -1, 0) + sides(field) - 4.0 * field
        speed = speed + step_dt * (stiff * lapl + press - damping * speed)
        field = field + step_dt * speed
    field = field[width : width + line_count]
    speed = speed[width : width + line_count]

    outgoing = jnp.dot(chooser.T, field, precision=high)
    x_tilde = lax.all_to_all(outgoing, "tile", split_axis=0, concat_axis=0, tiled=True)
    resid = (mask[:, None] * (x_tilde - iterate)).astype(jnp.bfloat16).reshape(-1)
    inner = tree_sum(jnp.dot(cols, resid, preferred_element_type=jnp.float32), "tile")
    rhs_cur = inner[:n_cur]
    rhs_past = inner[n_cur:]
    coeff = -solve_spd(inv_cur, rhs_cur)
    projected = rhs_past + jnp.dot(cross, coeff, precision=high)
    past = solve_spd(inv_past, projected)
    upd_cur = jnp.dot(
        coeff.astype(jnp.bfloat16),
        step_cur.reshape(step_cur.shape[0], -1),
        preferred_element_type=jnp.float32,
    )
    upd_past = jnp.dot(
        past.astype(jnp.bfloat16),
        step_past.reshape(step_past.shape[0], -1),
        preferred_element_type=jnp.float32,
    )
    update = (upd_cur - upd_past).reshape(x_tilde.shape)
    new_iterate = mask[:, None] * (x_tilde + update)
    return (new_iterate, field, speed)


def solution(mesh):
    placed = (
        P(("runs", "tile"), None),
        P(("runs", "tile"), None),
        P(("runs", "tile"), None),
        P(("runs", "tile"), None),
        P(("runs", "tile"), None),
        P(("runs", "tile"), None),
        P(None, ("runs", "tile"), None),
        P(None, ("runs", "tile"), None),
        P(None, ("runs", "tile"), None),
        P(None, ("runs", "tile"), None),
    )
    return jax.shard_map(
        local,
        mesh=mesh,
        in_specs=placed,
        out_specs=(P(("runs", "tile"), None), P(("runs", "tile"), None), P(("runs", "tile"), None)),
        check_vma=False,
    )
```

```python
import jax
import jax.numpy as jnp
from jax import lax
from jax.sharding import PartitionSpec as P


SUBSTEPS = 4


step_dt = 1.0
damping = 0.05


def tree_sum(value, axis):
    count = lax.axis_size(axis)
    if count & (count - 1):
        return lax.psum(value, axis)
    stride = 1
    while stride < count:
        value = value + lax.ppermute(value, axis, [(i, i ^ stride) for i in range(count)])
        stride *= 2
    return value


def halo_pair(cells, width, axis):
    count = lax.axis_size(axis)
    below = lax.ppermute(cells[-width:], axis, [(i, (i + 1) % count) for i in range(count)])
    above = lax.ppermute(cells[:width], axis, [((i + 1) % count, i) for i in range(count)])
    return below, above


def sides(center):
    zero_col = jnp.zeros((center.shape[0], 1), jnp.float32)
    left = jnp.concatenate([zero_col, center[:, :-1]], 1)
    right = jnp.concatenate([center[:, 1:], zero_col], 1)
    return left + right


def inverse_factor(matrix):
    factor = jnp.linalg.cholesky(matrix)
    eye = jnp.eye(matrix.shape[0], dtype=matrix.dtype)
    return lax.linalg.triangular_solve(factor, eye, left_side=True, lower=True)


def solve_spd(inverse, vector):
    high = lax.Precision.HIGHEST
    inner = jnp.dot(inverse, vector, precision=high)
    return jnp.dot(inverse.T, inner, precision=high)


def body(
    fluid_press,
    iterate,
    displace,
    velocity,
    stiffness,
    owners,
    diff_cur,
    step_cur,
    diff_past,
    step_past,
):
    high = lax.Precision.HIGHEST
    tile_count = lax.axis_size("tile")
    line_count = displace.shape[0]
    slot_count = iterate.shape[0]
    per_pair = slot_count // tile_count
    n_cur = diff_cur.shape[0]
    owner_list = owners[:, 0]
    onehot = (owner_list[:, None] == jnp.arange(tile_count, dtype=jnp.int32)[None, :]).astype(
        jnp.float32
    )
    below = (jnp.arange(line_count)[:, None] > jnp.arange(line_count)[None, :]).astype(jnp.float32)
    earlier = jnp.dot(below, onehot, precision=high)
    rank_in = jnp.sum(earlier * onehot, axis=1).astype(jnp.int32)
    slot_of = owner_list * per_pair + rank_in
    chooser = (slot_of[:, None] == jnp.arange(slot_count, dtype=jnp.int32)[None, :]).astype(
        jnp.float32
    )
    flags = jnp.sum(chooser, axis=0)
    lanes = fluid_press.shape[1]
    width = SUBSTEPS

    edge = jnp.concatenate([displace, velocity, stiffness], axis=1)
    edge_below, edge_above = halo_pair(edge, width, "tile")

    flag_rows = jnp.zeros((tile_count, 1, lanes), jnp.float32)
    flag_rows = flag_rows.at[:, 0, :per_pair].set(flags.reshape(tile_count, per_pair))
    sent = jnp.concatenate([fluid_press.reshape(tile_count, per_pair, lanes), flag_rows], axis=1)
    got = lax.all_to_all(sent, "tile", split_axis=0, concat_axis=0, tiled=True)
    returned = got[:, :per_pair, :].reshape(slot_count, lanes)
    mask = got[:, per_pair, :per_pair].reshape(slot_count)
    mask_half = mask.astype(jnp.bfloat16)

    cols = jnp.concatenate(
        [
            (diff_cur * mask_half[None, :, None]).reshape(n_cur, -1),
            (diff_past * mask_half[None, :, None]).reshape(diff_past.shape[0], -1),
        ],
        axis=0,
    )
    gram = lax.dot_general(cols, cols, (((1,), (1,)), ((), ())), preferred_element_type=jnp.float32)
    gram = tree_sum(gram, "tile")
    cross = gram[n_cur:, :n_cur]
    inv_cur = inverse_factor(gram[:n_cur, :n_cur])
    inv_past = inverse_factor(gram[n_cur:, n_cur:])

    pressure = jnp.dot(chooser, returned, precision=high)
    press_below, press_above = halo_pair(pressure, width, "tile")
    packed = jnp.concatenate(
        [
            jnp.concatenate([edge_below, press_below], axis=1),
            jnp.concatenate([edge, pressure], axis=1),
            jnp.concatenate([edge_above, press_above], axis=1),
        ],
        axis=0,
    )
    field = packed[:, :lanes]
    speed = packed[:, lanes : 2 * lanes]
    stiff = packed[:, 2 * lanes : 3 * lanes]
    press = packed[:, 3 * lanes :]
    for _ in range(SUBSTEPS):
        lapl = jnp.roll(field, 1, 0) + jnp.roll(field, -1, 0) + sides(field) - 4.0 * field
        speed = speed + step_dt * (stiff * lapl + press - damping * speed)
        field = field + step_dt * speed
    field = field[width : width + line_count]
    speed = speed[width : width + line_count]

    outgoing = jnp.dot(chooser.T, field, precision=high)
    x_tilde = lax.all_to_all(outgoing, "tile", split_axis=0, concat_axis=0, tiled=True)
    resid = (mask[:, None] * (x_tilde - iterate)).astype(jnp.bfloat16).reshape(-1)
    inner = tree_sum(jnp.dot(cols, resid, preferred_element_type=jnp.float32), "tile")
    rhs_cur = inner[:n_cur]
    rhs_past = inner[n_cur:]
    coeff = -solve_spd(inv_cur, rhs_cur)
    projected = rhs_past + jnp.dot(cross, coeff, precision=high)
    past = solve_spd(inv_past, projected)
    upd_cur = jnp.dot(
        coeff.astype(jnp.bfloat16),
        step_cur.reshape(step_cur.shape[0], -1),
        preferred_element_type=jnp.float32,
    )
    upd_past = jnp.dot(
        past.astype(jnp.bfloat16),
        step_past.reshape(step_past.shape[0], -1),
        preferred_element_type=jnp.float32,
    )
    update = (upd_cur - upd_past).reshape(x_tilde.shape)
    new_iterate = mask[:, None] * (x_tilde + update)
    return (new_iterate, field, speed)


def solution(mesh):
    placed = (
        P(("runs", "tile"), None),
        P(("runs", "tile"), None),
        P(("runs", "tile"), None),
        P(("runs", "tile"), None),
        P(("runs", "tile"), None),
        P(("runs", "tile"), None),
        P(None, ("runs", "tile"), None),
        P(None, ("runs", "tile"), None),
        P(None, ("runs", "tile"), None),
        P(None, ("runs", "tile"), None),
    )
    return jax.shard_map(
        body,
        mesh=mesh,
        in_specs=placed,
        out_specs=(P(("runs", "tile"), None), P(("runs", "tile"), None), P(("runs", "tile"), None)),
        check_vma=False,
    )
```

```python
import jax
import jax.numpy as jnp
from jax import lax
from jax.sharding import PartitionSpec as P

SUBSTEPS = 4


step_dt = 1.0
damping = 0.05


def tree_sum(value, axis):
    count = lax.axis_size(axis)
    if count & (count - 1):
        return lax.psum(value, axis)
    stride = 1
    while stride < count:
        value = value + lax.ppermute(value, axis, [(i, i ^ stride) for i in range(count)])
        stride *= 2
    return value


def halo_pair(cells, width, axis):
    count = lax.axis_size(axis)
    below = lax.ppermute(cells[-width:], axis, [(i, (i + 1) % count) for i in range(count)])
    above = lax.ppermute(cells[:width], axis, [((i + 1) % count, i) for i in range(count)])
    return below, above


def sides(center):
    zero_col = jnp.zeros((center.shape[0], 1), jnp.float32)
    left = jnp.concatenate([zero_col, center[:, :-1]], 1)
    right = jnp.concatenate([center[:, 1:], zero_col], 1)
    return left + right


def inverse_factor(matrix):
    factor = jnp.linalg.cholesky(matrix)
    eye = jnp.eye(matrix.shape[0], dtype=matrix.dtype)
    return lax.linalg.triangular_solve(factor, eye, left_side=True, lower=True)


def solve_spd(inverse, vector):
    high = lax.Precision.HIGHEST
    inner = jnp.dot(inverse, vector, precision=high)
    return jnp.dot(inverse.T, inner, precision=high)


def body(
    fluid_press,
    iterate,
    displace,
    velocity,
    stiffness,
    owners,
    diff_cur,
    step_cur,
    diff_past,
    step_past,
):
    high = lax.Precision.HIGHEST
    tile_count = lax.axis_size("tile")
    line_count = displace.shape[0]
    slot_count = iterate.shape[0]
    per_pair = slot_count // tile_count
    n_cur = diff_cur.shape[0]
    owner_list = owners[:, 0]
    onehot = (owner_list[:, None] == jnp.arange(tile_count, dtype=jnp.int32)[None, :]).astype(
        jnp.float32
    )
    below = (jnp.arange(line_count)[:, None] > jnp.arange(line_count)[None, :]).astype(jnp.float32)
    earlier = jnp.dot(below, onehot, precision=high)
    rank_in = jnp.sum(earlier * onehot, axis=1).astype(jnp.int32)
    slot_of = owner_list * per_pair + rank_in
    chooser = (slot_of[:, None] == jnp.arange(slot_count, dtype=jnp.int32)[None, :]).astype(
        jnp.float32
    )
    flags = jnp.sum(chooser, axis=0)
    lanes = fluid_press.shape[1]
    width = SUBSTEPS

    edge = jnp.concatenate([displace, velocity, stiffness], axis=1)
    edge_below, edge_above = halo_pair(edge, width, "tile")

    flag_rows = jnp.zeros((tile_count, 1, lanes), jnp.float32)
    flag_rows = flag_rows.at[:, 0, :per_pair].set(flags.reshape(tile_count, per_pair))
    sent = jnp.concatenate([fluid_press.reshape(tile_count, per_pair, lanes), flag_rows], axis=1)
    got = lax.all_to_all(sent, "tile", split_axis=0, concat_axis=0, tiled=True)
    returned = got[:, :per_pair, :].reshape(slot_count, lanes)
    mask = got[:, per_pair, :per_pair].reshape(slot_count)
    mask_half = mask.astype(jnp.bfloat16)

    both = (((1, 2), (1, 2)), ((), ()))
    cur_half = diff_cur * mask_half[None, :, None]
    past_half = diff_past * mask_half[None, :, None]
    gram_cur = lax.dot_general(cur_half, diff_cur, both, preferred_element_type=jnp.float32)
    gram_past = lax.dot_general(past_half, diff_past, both, preferred_element_type=jnp.float32)
    cross = lax.dot_general(past_half, diff_cur, both, preferred_element_type=jnp.float32)
    n_past = diff_past.shape[0]
    summed = tree_sum(
        jnp.concatenate([gram_cur.reshape(-1), gram_past.reshape(-1), cross.reshape(-1)]), "tile"
    )
    gram_cur = summed[: n_cur * n_cur].reshape(n_cur, n_cur)
    gram_past = summed[n_cur * n_cur : n_cur * n_cur + n_past * n_past].reshape(n_past, n_past)
    cross = summed[n_cur * n_cur + n_past * n_past :].reshape(n_past, n_cur)
    blocks = jnp.zeros((n_cur + n_past, n_cur + n_past), jnp.float32)
    blocks = blocks.at[:n_cur, :n_cur].set(gram_cur).at[n_cur:, n_cur:].set(gram_past)
    inverse = inverse_factor(blocks)
    inv_cur = inverse[:n_cur, :n_cur]
    inv_past = inverse[n_cur:, n_cur:]

    pressure = jnp.dot(chooser, returned, precision=high)
    press_below, press_above = halo_pair(pressure, width, "tile")
    packed = jnp.concatenate(
        [
            jnp.concatenate([edge_below, press_below], axis=1),
            jnp.concatenate([edge, pressure], axis=1),
            jnp.concatenate([edge_above, press_above], axis=1),
        ],
        axis=0,
    )
    field = packed[:, :lanes]
    speed = packed[:, lanes : 2 * lanes]
    stiff = packed[:, 2 * lanes : 3 * lanes]
    press = packed[:, 3 * lanes :]
    for _ in range(SUBSTEPS):
        lapl = jnp.roll(field, 1, 0) + jnp.roll(field, -1, 0) + sides(field) - 4.0 * field
        speed = speed + step_dt * (stiff * lapl + press - damping * speed)
        field = field + step_dt * speed
    field = field[width : width + line_count]
    speed = speed[width : width + line_count]

    outgoing = jnp.dot(chooser.T, field, precision=high)
    x_tilde = lax.all_to_all(outgoing, "tile", split_axis=0, concat_axis=0, tiled=True)
    resid = (mask[:, None] * (x_tilde - iterate)).astype(jnp.bfloat16)
    lhs = (((1, 2), (0, 1)), ((), ()))
    inner = jnp.concatenate(
        [
            lax.dot_general(diff_cur, resid, lhs, preferred_element_type=jnp.float32),
            lax.dot_general(diff_past, resid, lhs, preferred_element_type=jnp.float32),
        ]
    )
    inner = tree_sum(inner, "tile")
    rhs_cur = inner[:n_cur]
    rhs_past = inner[n_cur:]
    coeff = -solve_spd(inv_cur, rhs_cur)
    projected = rhs_past + jnp.dot(cross, coeff, precision=high)
    past = solve_spd(inv_past, projected)
    upd_cur = jnp.dot(
        coeff.astype(jnp.bfloat16),
        step_cur.reshape(step_cur.shape[0], -1),
        preferred_element_type=jnp.float32,
    )
    upd_past = jnp.dot(
        past.astype(jnp.bfloat16),
        step_past.reshape(step_past.shape[0], -1),
        preferred_element_type=jnp.float32,
    )
    update = (upd_cur - upd_past).reshape(x_tilde.shape)
    new_iterate = mask[:, None] * (x_tilde + update)
    return (new_iterate, field, speed)


def solution(mesh):
    placed = (
        P(("runs", "tile"), None),
        P(("runs", "tile"), None),
        P(("runs", "tile"), None),
        P(("runs", "tile"), None),
        P(("runs", "tile"), None),
        P(("runs", "tile"), None),
        P(None, ("runs", "tile"), None),
        P(None, ("runs", "tile"), None),
        P(None, ("runs", "tile"), None),
        P(None, ("runs", "tile"), None),
    )
    return jax.shard_map(
        body,
        mesh=mesh,
        in_specs=placed,
        out_specs=(P(("runs", "tile"), None), P(("runs", "tile"), None), P(("runs", "tile"), None)),
        check_vma=False,
    )
```

```python
import jax
import jax.numpy as jnp
from jax import lax
from jax.sharding import PartitionSpec as P


SUBSTEPS = 4


step_dt = 1.0
damping = 0.05


def tree_sum(value, axis):
    count = lax.axis_size(axis)
    if count & (count - 1):
        return lax.psum(value, axis)
    stride = 1
    while stride < count:
        value = value + lax.ppermute(value, axis, [(i, i ^ stride) for i in range(count)])
        stride *= 2
    return value


def halo_pair(parts, width, axis):
    count = lax.axis_size(axis)
    tail = jnp.concatenate([part[-width:] for part in parts], axis=1)
    head = jnp.concatenate([part[:width] for part in parts], axis=1)
    below = lax.ppermute(tail, axis, [(i, (i + 1) % count) for i in range(count)])
    above = lax.ppermute(head, axis, [((i + 1) % count, i) for i in range(count)])
    return below, above


def sides(center):
    zero_col = jnp.zeros((center.shape[0], 1), jnp.float32)
    left = jnp.concatenate([zero_col, center[:, :-1]], 1)
    right = jnp.concatenate([center[:, 1:], zero_col], 1)
    return left + right


def inverse_factor(matrix):
    factor = jnp.linalg.cholesky(matrix)
    eye = jnp.eye(matrix.shape[0], dtype=matrix.dtype)
    return lax.linalg.triangular_solve(factor, eye, left_side=True, lower=True)


def solve_spd(inverse, vector):
    high = lax.Precision.HIGHEST
    inner = jnp.dot(inverse, vector, precision=high)
    return jnp.dot(inverse.T, inner, precision=high)


def body(
    fluid_press,
    iterate,
    displace,
    velocity,
    stiffness,
    owners,
    diff_cur,
    step_cur,
    diff_past,
    step_past,
):
    high = lax.Precision.HIGHEST
    tile_count = lax.axis_size("tile")
    line_count = displace.shape[0]
    slot_count = iterate.shape[0]
    per_pair = slot_count // tile_count
    n_cur = diff_cur.shape[0]
    owner_list = owners[:, 0]
    onehot = (owner_list[:, None] == jnp.arange(tile_count, dtype=jnp.int32)[None, :]).astype(
        jnp.float32
    )
    below = (jnp.arange(line_count)[:, None] > jnp.arange(line_count)[None, :]).astype(jnp.float32)
    earlier = jnp.dot(below, onehot, precision=high)
    rank_in = jnp.sum(earlier * onehot, axis=1).astype(jnp.int32)
    slot_of = owner_list * per_pair + rank_in
    chooser = (slot_of[:, None] == jnp.arange(slot_count, dtype=jnp.int32)[None, :]).astype(
        jnp.float32
    )
    flags = jnp.sum(chooser, axis=0)
    lanes = fluid_press.shape[1]
    width = SUBSTEPS

    edge_below, edge_above = halo_pair((displace, velocity, stiffness), width, "tile")

    flag_rows = jnp.zeros((tile_count, 1, lanes), jnp.float32)
    flag_rows = flag_rows.at[:, 0, :per_pair].set(flags.reshape(tile_count, per_pair))
    sent = jnp.concatenate([fluid_press.reshape(tile_count, per_pair, lanes), flag_rows], axis=1)
    got = lax.all_to_all(sent, "tile", split_axis=0, concat_axis=0, tiled=True)
    returned = got[:, :per_pair, :].reshape(slot_count, lanes)
    mask = got[:, per_pair, :per_pair].reshape(slot_count)
    mask_half = mask.astype(jnp.bfloat16)

    cols = jnp.concatenate(
        [
            (diff_cur * mask_half[None, :, None]).reshape(n_cur, -1),
            (diff_past * mask_half[None, :, None]).reshape(diff_past.shape[0], -1),
        ],
        axis=0,
    )
    gram = lax.dot_general(cols, cols, (((1,), (1,)), ((), ())), preferred_element_type=jnp.float32)
    gram = tree_sum(gram, "tile")
    cross = gram[n_cur:, :n_cur]
    inv_cur = inverse_factor(gram[:n_cur, :n_cur])
    inv_past = inverse_factor(gram[n_cur:, n_cur:])

    pressure = jnp.dot(chooser, returned, precision=high)
    press_below, press_above = halo_pair((pressure,), width, "tile")

    def extended(middle, which):
        cut = slice(which * lanes, (which + 1) * lanes)
        return jnp.concatenate([edge_below[:, cut], middle, edge_above[:, cut]], axis=0)

    field = extended(displace, 0)
    speed = extended(velocity, 1)
    stiff = extended(stiffness, 2)
    press = jnp.concatenate([press_below, pressure, press_above], axis=0)
    for _ in range(SUBSTEPS):
        lapl = jnp.roll(field, 1, 0) + jnp.roll(field, -1, 0) + sides(field) - 4.0 * field
        speed = speed + step_dt * (stiff * lapl + press - damping * speed)
        field = field + step_dt * speed
    field = field[width : width + line_count]
    speed = speed[width : width + line_count]

    outgoing = jnp.dot(chooser.T, field, precision=high)
    x_tilde = lax.all_to_all(outgoing, "tile", split_axis=0, concat_axis=0, tiled=True)
    resid = (mask[:, None] * (x_tilde - iterate)).astype(jnp.bfloat16).reshape(-1)
    inner = tree_sum(jnp.dot(cols, resid, preferred_element_type=jnp.float32), "tile")
    rhs_cur = inner[:n_cur]
    rhs_past = inner[n_cur:]
    coeff = -solve_spd(inv_cur, rhs_cur)
    projected = rhs_past + jnp.dot(cross, coeff, precision=high)
    past = solve_spd(inv_past, projected)
    upd_cur = jnp.dot(
        coeff.astype(jnp.bfloat16),
        step_cur.reshape(step_cur.shape[0], -1),
        preferred_element_type=jnp.float32,
    )
    upd_past = jnp.dot(
        past.astype(jnp.bfloat16),
        step_past.reshape(step_past.shape[0], -1),
        preferred_element_type=jnp.float32,
    )
    update = (upd_cur - upd_past).reshape(x_tilde.shape)
    new_iterate = mask[:, None] * (x_tilde + update)
    return (new_iterate, field, speed)


def solution(mesh):
    placed = (
        P(("runs", "tile"), None),
        P(("runs", "tile"), None),
        P(("runs", "tile"), None),
        P(("runs", "tile"), None),
        P(("runs", "tile"), None),
        P(("runs", "tile"), None),
        P(None, ("runs", "tile"), None),
        P(None, ("runs", "tile"), None),
        P(None, ("runs", "tile"), None),
        P(None, ("runs", "tile"), None),
    )
    return jax.shard_map(
        body,
        mesh=mesh,
        in_specs=placed,
        out_specs=(P(("runs", "tile"), None), P(("runs", "tile"), None), P(("runs", "tile"), None)),
        check_vma=False,
    )
```

```python
import jax
import jax.numpy as jnp
from jax import lax
from jax.sharding import PartitionSpec as P

SUBSTEPS = 4


step_dt = 1.0
damping = 0.05


def tree_sum(value, axis):
    count = lax.axis_size(axis)
    if count & (count - 1):
        return lax.psum(value, axis)
    stride = 1
    while stride < count:
        value = value + lax.ppermute(value, axis, [(i, i ^ stride) for i in range(count)])
        stride *= 2
    return value


def halo_pair(cells, width, axis):
    count = lax.axis_size(axis)
    below = lax.ppermute(cells[-width:], axis, [(i, (i + 1) % count) for i in range(count)])
    above = lax.ppermute(cells[:width], axis, [((i + 1) % count, i) for i in range(count)])
    return below, above


def to_half(value):
    return lax.reduce_precision(value, exponent_bits=8, mantissa_bits=7)


def sides(center):
    zero_col = jnp.zeros((center.shape[0], 1), jnp.float32)
    left = jnp.concatenate([zero_col, center[:, :-1]], 1)
    right = jnp.concatenate([center[:, 1:], zero_col], 1)
    return left + right


def inverse_factor(matrix):
    factor = jnp.linalg.cholesky(matrix)
    eye = jnp.eye(matrix.shape[0], dtype=matrix.dtype)
    return lax.linalg.triangular_solve(factor, eye, left_side=True, lower=True)


def solve_spd(inverse, vector):
    high = lax.Precision.HIGHEST
    inner = jnp.dot(inverse, vector, precision=high)
    return jnp.dot(inverse.T, inner, precision=high)


def local(
    fluid_press,
    iterate,
    displace,
    velocity,
    stiffness,
    owners,
    diff_cur,
    step_cur,
    diff_past,
    step_past,
):
    high = lax.Precision.HIGHEST
    tile_count = lax.axis_size("tile")
    line_count = displace.shape[0]
    slot_count = iterate.shape[0]
    per_pair = slot_count // tile_count
    n_cur = diff_cur.shape[0]
    owner_list = owners[:, 0]
    onehot = (owner_list[:, None] == jnp.arange(tile_count, dtype=jnp.int32)[None, :]).astype(
        jnp.float32
    )
    below = (jnp.arange(line_count)[:, None] > jnp.arange(line_count)[None, :]).astype(jnp.float32)
    earlier = jnp.dot(below, onehot, precision=high)
    rank_in = jnp.sum(earlier * onehot, axis=1).astype(jnp.int32)
    slot_of = owner_list * per_pair + rank_in
    chooser = (slot_of[:, None] == jnp.arange(slot_count, dtype=jnp.int32)[None, :]).astype(
        jnp.float32
    )
    flags = jnp.sum(chooser, axis=0)
    lanes = fluid_press.shape[1]
    width = SUBSTEPS

    edge = jnp.concatenate([displace, velocity, stiffness], axis=1)
    edge_below, edge_above = halo_pair(edge, width, "tile")

    flag_rows = jnp.zeros((tile_count, 1, lanes), jnp.float32)
    flag_rows = flag_rows.at[:, 0, :per_pair].set(flags.reshape(tile_count, per_pair))
    sent = jnp.concatenate([fluid_press.reshape(tile_count, per_pair, lanes), flag_rows], axis=1)
    got = lax.all_to_all(sent, "tile", split_axis=0, concat_axis=0, tiled=True)
    returned = got[:, :per_pair, :].reshape(slot_count, lanes)
    mask = got[:, per_pair, :per_pair].reshape(slot_count)
    mask_half = mask.astype(jnp.bfloat16)

    cols = jnp.concatenate(
        [
            (diff_cur * mask_half[None, :, None]).reshape(n_cur, -1),
            (diff_past * mask_half[None, :, None]).reshape(diff_past.shape[0], -1),
        ],
        axis=0,
    )
    gram = lax.dot_general(cols, cols, (((1,), (1,)), ((), ())), preferred_element_type=jnp.float32)
    gram = tree_sum(gram, "tile")
    cross = gram[n_cur:, :n_cur]
    inv_cur = inverse_factor(gram[:n_cur, :n_cur])
    inv_past = inverse_factor(gram[n_cur:, n_cur:])

    pressure = jnp.dot(chooser, returned, precision=high)
    press_below, press_above = halo_pair(pressure, width, "tile")
    packed = jnp.concatenate(
        [
            jnp.concatenate([edge_below, press_below], axis=1),
            jnp.concatenate([edge, pressure], axis=1),
            jnp.concatenate([edge_above, press_above], axis=1),
        ],
        axis=0,
    )
    field = packed[:, :lanes]
    speed = packed[:, lanes : 2 * lanes]
    stiff = packed[:, 2 * lanes : 3 * lanes]
    press = packed[:, 3 * lanes :]
    for substep in range(SUBSTEPS):
        lapl = jnp.roll(field, 1, 0) + jnp.roll(field, -1, 0) + sides(field) - 4.0 * field
        speed = speed + step_dt * (stiff * lapl + press - damping * speed)
        field = field + step_dt * speed
    field = field[width : width + line_count]
    speed = speed[width : width + line_count]

    outgoing = jnp.dot(chooser.T, field, precision=high)
    x_tilde = lax.all_to_all(outgoing, "tile", split_axis=0, concat_axis=0, tiled=True)
    resid = to_half(mask[:, None] * (x_tilde - iterate))
    inner = jnp.concatenate(
        [
            jnp.sum(diff_cur.astype(jnp.float32) * resid[None], axis=(1, 2)),
            jnp.sum(diff_past.astype(jnp.float32) * resid[None], axis=(1, 2)),
        ]
    )
    inner = tree_sum(inner, "tile")
    rhs_cur = inner[:n_cur]
    rhs_past = inner[n_cur:]
    coeff = -solve_spd(inv_cur, rhs_cur)
    projected = rhs_past + jnp.dot(cross, coeff, precision=high)
    past = solve_spd(inv_past, projected)
    coeff_half = to_half(coeff)
    past_half = to_half(past)
    upd_cur = jnp.sum(coeff_half[:, None, None] * step_cur.astype(jnp.float32), axis=0)
    upd_past = jnp.sum(past_half[:, None, None] * step_past.astype(jnp.float32), axis=0)
    update = upd_cur - upd_past
    new_iterate = mask[:, None] * (x_tilde + update)
    return (new_iterate, field, speed)


def solution(mesh):
    placed = (
        P(("runs", "tile"), None),
        P(("runs", "tile"), None),
        P(("runs", "tile"), None),
        P(("runs", "tile"), None),
        P(("runs", "tile"), None),
        P(("runs", "tile"), None),
        P(None, ("runs", "tile"), None),
        P(None, ("runs", "tile"), None),
        P(None, ("runs", "tile"), None),
        P(None, ("runs", "tile"), None),
    )
    return jax.shard_map(
        local,
        mesh=mesh,
        in_specs=placed,
        out_specs=(P(("runs", "tile"), None), P(("runs", "tile"), None), P(("runs", "tile"), None)),
        check_vma=False,
    )
```

```python
import jax
import jax.numpy as jnp
from jax import lax
from jax.sharding import PartitionSpec as P


SUBSTEPS = 4


step_dt = 1.0
damping = 0.05


def tree_sum(value, axis):
    count = lax.axis_size(axis)
    if count & (count - 1):
        return lax.psum(value, axis)
    stride = 1
    while stride < count:
        value = value + lax.ppermute(value, axis, [(i, i ^ stride) for i in range(count)])
        stride *= 2
    return value


def halo_pair(cells, width, axis):
    count = lax.axis_size(axis)
    below = lax.ppermute(cells[-width:], axis, [(i, (i + 1) % count) for i in range(count)])
    above = lax.ppermute(cells[:width], axis, [((i + 1) % count, i) for i in range(count)])
    return below, above


def to_half(value):
    return lax.reduce_precision(value, exponent_bits=8, mantissa_bits=7)


def sides(center):
    zero_col = jnp.zeros((center.shape[0], 1), jnp.float32)
    left = jnp.concatenate([zero_col, center[:, :-1]], 1)
    right = jnp.concatenate([center[:, 1:], zero_col], 1)
    return left + right


def inverse_factor(matrix):
    factor = jnp.linalg.cholesky(matrix)
    eye = jnp.eye(matrix.shape[0], dtype=matrix.dtype)
    return lax.linalg.triangular_solve(factor, eye, left_side=True, lower=True)


def solve_spd(inverse, vector):
    high = lax.Precision.HIGHEST
    inner = jnp.dot(inverse, vector, precision=high)
    return jnp.dot(inverse.T, inner, precision=high)


def body(
    fluid_press,
    iterate,
    displace,
    velocity,
    stiffness,
    owners,
    diff_cur,
    step_cur,
    diff_past,
    step_past,
):
    high = lax.Precision.HIGHEST
    tile_count = lax.axis_size("tile")
    line_count = displace.shape[0]
    slot_count = iterate.shape[0]
    per_pair = slot_count // tile_count
    n_cur = diff_cur.shape[0]
    owner_list = owners[:, 0]
    onehot = (owner_list[:, None] == jnp.arange(tile_count, dtype=jnp.int32)[None, :]).astype(
        jnp.float32
    )
    below = (jnp.arange(line_count)[:, None] > jnp.arange(line_count)[None, :]).astype(jnp.float32)
    earlier = jnp.dot(below, onehot, precision=high)
    rank_in = jnp.sum(earlier * onehot, axis=1).astype(jnp.int32)
    slot_of = owner_list * per_pair + rank_in
    chooser = (slot_of[:, None] == jnp.arange(slot_count, dtype=jnp.int32)[None, :]).astype(
        jnp.float32
    )
    flags = jnp.sum(chooser, axis=0)
    lanes = fluid_press.shape[1]
    width = SUBSTEPS

    edge = jnp.concatenate([displace, velocity, stiffness], axis=1)
    edge_below, edge_above = halo_pair(edge, width, "tile")

    flag_rows = jnp.zeros((tile_count, 1, lanes), jnp.float32)
    flag_rows = flag_rows.at[:, 0, :per_pair].set(flags.reshape(tile_count, per_pair))
    sent = jnp.concatenate([fluid_press.reshape(tile_count, per_pair, lanes), flag_rows], axis=1)
    got = lax.all_to_all(sent, "tile", split_axis=0, concat_axis=0, tiled=True)
    returned = got[:, :per_pair, :].reshape(slot_count, lanes)
    mask = got[:, per_pair, :per_pair].reshape(slot_count)
    mask_half = mask.astype(jnp.bfloat16)

    cols = jnp.concatenate(
        [
            (diff_cur * mask_half[None, :, None]).reshape(n_cur, -1),
            (diff_past * mask_half[None, :, None]).reshape(diff_past.shape[0], -1),
        ],
        axis=0,
    )
    gram = lax.dot_general(cols, cols, (((1,), (1,)), ((), ())), preferred_element_type=jnp.float32)
    gram = tree_sum(gram, "tile")
    cross = gram[n_cur:, :n_cur]
    inv_cur = inverse_factor(gram[:n_cur, :n_cur])
    inv_past = inverse_factor(gram[n_cur:, n_cur:])

    pressure = jnp.dot(chooser, returned, precision=high)
    press_below, press_above = halo_pair(pressure, width, "tile")
    packed = jnp.concatenate(
        [
            jnp.concatenate([edge_below, press_below], axis=1),
            jnp.concatenate([edge, pressure], axis=1),
            jnp.concatenate([edge_above, press_above], axis=1),
        ],
        axis=0,
    )
    field = packed[:, :lanes]
    speed = packed[:, lanes : 2 * lanes]
    stiff = packed[:, 2 * lanes : 3 * lanes]
    press = packed[:, 3 * lanes :]
    for _ in range(SUBSTEPS):
        lapl = jnp.roll(field, 1, 0) + jnp.roll(field, -1, 0) + sides(field) - 4.0 * field
        speed = speed + step_dt * (stiff * lapl + press - damping * speed)
        field = field + step_dt * speed
    field = field[width : width + line_count]
    speed = speed[width : width + line_count]

    outgoing = jnp.dot(chooser.T, field, precision=high)
    x_tilde = lax.all_to_all(outgoing, "tile", split_axis=0, concat_axis=0, tiled=True)
    resid = to_half(mask[:, None] * (x_tilde - iterate))
    inner = jnp.concatenate(
        [
            jnp.sum(diff_cur.astype(jnp.float32) * resid[None], axis=(1, 2)),
            jnp.sum(diff_past.astype(jnp.float32) * resid[None], axis=(1, 2)),
        ]
    )
    inner = tree_sum(inner, "tile")
    rhs_cur = inner[:n_cur]
    rhs_past = inner[n_cur:]
    coeff = -solve_spd(inv_cur, rhs_cur)
    projected = rhs_past + jnp.dot(cross, coeff, precision=high)
    past = solve_spd(inv_past, projected)
    coeff_half = to_half(coeff)
    past_half = to_half(past)
    upd_cur = jnp.sum(coeff_half[:, None, None] * step_cur.astype(jnp.float32), axis=0)
    upd_past = jnp.sum(past_half[:, None, None] * step_past.astype(jnp.float32), axis=0)
    update = upd_cur - upd_past
    new_iterate = mask[:, None] * (x_tilde + update)
    return (new_iterate, field, speed)


def solution(mesh):
    placed = (
        P(("runs", "tile"), None),
        P(("runs", "tile"), None),
        P(("runs", "tile"), None),
        P(("runs", "tile"), None),
        P(("runs", "tile"), None),
        P(("runs", "tile"), None),
        P(None, ("runs", "tile"), None),
        P(None, ("runs", "tile"), None),
        P(None, ("runs", "tile"), None),
        P(None, ("runs", "tile"), None),
    )
    return jax.shard_map(
        body,
        mesh=mesh,
        in_specs=placed,
        out_specs=(P(("runs", "tile"), None), P(("runs", "tile"), None), P(("runs", "tile"), None)),
        check_vma=False,
    )
```

```python
import jax
import jax.numpy as jnp
from jax import lax
from jax.experimental import pallas as pl
from jax.sharding import PartitionSpec as P


SUBSTEPS = 4


step_dt = 1.0
damping = 0.05


def tree_sum(value, axis):
    count = lax.axis_size(axis)
    if count & (count - 1):
        return lax.psum(value, axis)
    stride = 1
    while stride < count:
        value = value + lax.ppermute(value, axis, [(i, i ^ stride) for i in range(count)])
        stride *= 2
    return value


def halo_pair(cells, width, axis):
    count = lax.axis_size(axis)
    below = lax.ppermute(cells[-width:], axis, [(i, (i + 1) % count) for i in range(count)])
    above = lax.ppermute(cells[:width], axis, [((i + 1) % count, i) for i in range(count)])
    return below, above


def to_half(value):
    return lax.reduce_precision(value, exponent_bits=8, mantissa_bits=7)


def sides(center):
    zero_col = jnp.zeros((center.shape[0], 1), jnp.float32)
    left = jnp.concatenate([zero_col, center[:, :-1]], 1)
    right = jnp.concatenate([center[:, 1:], zero_col], 1)
    return left + right


def eliminate(a):
    n = a.shape[0]
    rows = lax.broadcasted_iota(jnp.int32, (n, n), 0)
    cols = lax.broadcasted_iota(jnp.int32, (n, n), 1)
    m = jnp.where(rows == cols, 1.0, 0.0).astype(jnp.float32)
    for j in range(n):
        on_row = rows == j
        row = jnp.sum(jnp.where(on_row, a, 0.0), axis=0, keepdims=True)
        col = jnp.sum(jnp.where(cols == j, a, 0.0), axis=1, keepdims=True)
        pivot = jnp.sum(jnp.where(cols[:1] == j, row, 0.0), axis=1, keepdims=True)
        scale = 1.0 / jnp.sqrt(pivot)
        row = jnp.where(cols[:1] >= j, row * scale, 0.0)
        lower = jnp.where(rows[:, :1] > j, col * scale, 0.0)
        m_row = jnp.sum(jnp.where(on_row, m, 0.0), axis=0, keepdims=True) * scale
        a = jnp.where(on_row, row, a - lower * row)
        m = jnp.where(on_row, m_row, m - lower * m_row)
    return m


def factor_kernel(cur_ref, past_ref, inv_cur_ref, inv_past_ref):
    inv_cur_ref[...] = eliminate(cur_ref[...])
    inv_past_ref[...] = eliminate(past_ref[...])


def inverse_factors(cur, past):
    shapes = (jax.ShapeDtypeStruct(cur.shape, jnp.float32), jax.ShapeDtypeStruct(past.shape, jnp.float32))
    return pl.pallas_call(factor_kernel, out_shape=shapes)(cur, past)


def solve_spd(inverse, vector):
    high = lax.Precision.HIGHEST
    inner = jnp.dot(inverse, vector, precision=high)
    return jnp.dot(inverse.T, inner, precision=high)


def body(
    fluid_press,
    iterate,
    displace,
    velocity,
    stiffness,
    owners,
    diff_cur,
    step_cur,
    diff_past,
    step_past,
):
    high = lax.Precision.HIGHEST
    tile_count = lax.axis_size("tile")
    line_count = displace.shape[0]
    slot_count = iterate.shape[0]
    per_pair = slot_count // tile_count
    n_cur = diff_cur.shape[0]
    owner_list = owners[:, 0]
    onehot = (owner_list[:, None] == jnp.arange(tile_count, dtype=jnp.int32)[None, :]).astype(
        jnp.float32
    )
    below = (jnp.arange(line_count)[:, None] > jnp.arange(line_count)[None, :]).astype(jnp.float32)
    earlier = jnp.dot(below, onehot, precision=high)
    rank_in = jnp.sum(earlier * onehot, axis=1).astype(jnp.int32)
    slot_of = owner_list * per_pair + rank_in
    chooser = (slot_of[:, None] == jnp.arange(slot_count, dtype=jnp.int32)[None, :]).astype(
        jnp.float32
    )
    flags = jnp.sum(chooser, axis=0)
    lanes = fluid_press.shape[1]
    width = SUBSTEPS

    edge = jnp.concatenate([displace, velocity, stiffness], axis=1)
    edge_below, edge_above = halo_pair(edge, width, "tile")

    flag_rows = jnp.zeros((tile_count, 1, lanes), jnp.float32)
    flag_rows = flag_rows.at[:, 0, :per_pair].set(flags.reshape(tile_count, per_pair))
    sent = jnp.concatenate([fluid_press.reshape(tile_count, per_pair, lanes), flag_rows], axis=1)
    got = lax.all_to_all(sent, "tile", split_axis=0, concat_axis=0, tiled=True)
    returned = got[:, :per_pair, :].reshape(slot_count, lanes)
    mask = got[:, per_pair, :per_pair].reshape(slot_count)
    mask_half = mask.astype(jnp.bfloat16)

    cols = jnp.concatenate(
        [
            (diff_cur * mask_half[None, :, None]).reshape(n_cur, -1),
            (diff_past * mask_half[None, :, None]).reshape(diff_past.shape[0], -1),
        ],
        axis=0,
    )
    gram = lax.dot_general(cols, cols, (((1,), (1,)), ((), ())), preferred_element_type=jnp.float32)
    gram = tree_sum(gram, "tile")
    cross = gram[n_cur:, :n_cur]
    inv_cur, inv_past = inverse_factors(gram[:n_cur, :n_cur], gram[n_cur:, n_cur:])

    pressure = jnp.dot(chooser, returned, precision=high)
    press_below, press_above = halo_pair(pressure, width, "tile")
    packed = jnp.concatenate(
        [
            jnp.concatenate([edge_below, press_below], axis=1),
            jnp.concatenate([edge, pressure], axis=1),
            jnp.concatenate([edge_above, press_above], axis=1),
        ],
        axis=0,
    )
    field = packed[:, :lanes]
    speed = packed[:, lanes : 2 * lanes]
    stiff = packed[:, 2 * lanes : 3 * lanes]
    press = packed[:, 3 * lanes :]
    for _ in range(SUBSTEPS):
        lapl = jnp.roll(field, 1, 0) + jnp.roll(field, -1, 0) + sides(field) - 4.0 * field
        speed = speed + step_dt * (stiff * lapl + press - damping * speed)
        field = field + step_dt * speed
    field = field[width : width + line_count]
    speed = speed[width : width + line_count]

    outgoing = jnp.dot(chooser.T, field, precision=high)
    x_tilde = lax.all_to_all(outgoing, "tile", split_axis=0, concat_axis=0, tiled=True)
    resid = to_half(mask[:, None] * (x_tilde - iterate))
    inner = jnp.concatenate(
        [
            jnp.sum(diff_cur.astype(jnp.float32) * resid[None], axis=(1, 2)),
            jnp.sum(diff_past.astype(jnp.float32) * resid[None], axis=(1, 2)),
        ]
    )
    inner = tree_sum(inner, "tile")
    rhs_cur = inner[:n_cur]
    rhs_past = inner[n_cur:]
    coeff = -solve_spd(inv_cur, rhs_cur)
    projected = rhs_past + jnp.dot(cross, coeff, precision=high)
    past = solve_spd(inv_past, projected)
    coeff_half = to_half(coeff)
    past_half = to_half(past)
    upd_cur = jnp.sum(coeff_half[:, None, None] * step_cur.astype(jnp.float32), axis=0)
    upd_past = jnp.sum(past_half[:, None, None] * step_past.astype(jnp.float32), axis=0)
    update = upd_cur - upd_past
    new_iterate = mask[:, None] * (x_tilde + update)
    return (new_iterate, field, speed)


def solution(mesh):
    placed = (
        P(("runs", "tile"), None),
        P(("runs", "tile"), None),
        P(("runs", "tile"), None),
        P(("runs", "tile"), None),
        P(("runs", "tile"), None),
        P(("runs", "tile"), None),
        P(None, ("runs", "tile"), None),
        P(None, ("runs", "tile"), None),
        P(None, ("runs", "tile"), None),
        P(None, ("runs", "tile"), None),
    )
    return jax.shard_map(
        body,
        mesh=mesh,
        in_specs=placed,
        out_specs=(P(("runs", "tile"), None), P(("runs", "tile"), None), P(("runs", "tile"), None)),
        check_vma=False,
    )
```

```python
import jax
import jax.numpy as jnp
from jax import lax
from jax.experimental import pallas as pl
from jax.sharding import PartitionSpec as P

SUBSTEPS = 4


step_dt = 1.0
damping = 0.05


def tree_sum(value, axis):
    count = lax.axis_size(axis)
    if count & (count - 1):
        return lax.psum(value, axis)
    stride = 1
    while stride < count:
        value = value + lax.ppermute(value, axis, [(i, i ^ stride) for i in range(count)])
        stride *= 2
    return value


def halo_pair(cells, width, axis):
    count = lax.axis_size(axis)
    below = lax.ppermute(cells[-width:], axis, [(i, (i + 1) % count) for i in range(count)])
    above = lax.ppermute(cells[:width], axis, [((i + 1) % count, i) for i in range(count)])
    return below, above


def to_half(value):
    return lax.reduce_precision(value, exponent_bits=8, mantissa_bits=7)


def sides(center):
    zero_col = jnp.zeros((center.shape[0], 1), jnp.float32)
    left = jnp.concatenate([zero_col, center[:, :-1]], 1)
    right = jnp.concatenate([center[:, 1:], zero_col], 1)
    return left + right


def eliminate(mats):
    state = []
    for a in mats:
        n = a.shape[0]
        rows = lax.broadcasted_iota(jnp.int32, (n, n), 0)
        cols = lax.broadcasted_iota(jnp.int32, (n, n), 1)
        state.append([a, jnp.where(rows == cols, 1.0, 0.0).astype(jnp.float32), rows, cols])
    for j in range(max(a.shape[0] for a in mats)):
        for item in state:
            a, m, rows, cols = item
            if j >= a.shape[0]:
                continue
            on_row = rows == j
            row = jnp.sum(jnp.where(on_row, a, 0.0), axis=0, keepdims=True)
            col = jnp.sum(jnp.where(cols == j, a, 0.0), axis=1, keepdims=True)
            pivot = jnp.sum(jnp.where(cols[:1] == j, row, 0.0), axis=1, keepdims=True)
            scale = 1.0 / jnp.sqrt(pivot)
            row = jnp.where(cols[:1] >= j, row * scale, 0.0)
            lower = jnp.where(rows[:, :1] > j, col * scale, 0.0)
            m_row = jnp.sum(jnp.where(on_row, m, 0.0), axis=0, keepdims=True) * scale
            item[0] = jnp.where(on_row, row, a - lower * row)
            item[1] = jnp.where(on_row, m_row, m - lower * m_row)
    return [item[1] for item in state]


def factor_kernel(cur_ref, past_ref, inv_cur_ref, inv_past_ref):
    inv_cur_ref[...], inv_past_ref[...] = eliminate([cur_ref[...], past_ref[...]])


def inverse_factors(cur, past):
    shapes = (jax.ShapeDtypeStruct(cur.shape, jnp.float32), jax.ShapeDtypeStruct(past.shape, jnp.float32))
    return pl.pallas_call(factor_kernel, out_shape=shapes)(cur, past)


def solve_spd(inverse, vector):
    high = lax.Precision.HIGHEST
    inner = jnp.dot(inverse, vector, precision=high)
    return jnp.dot(inverse.T, inner, precision=high)


def body(
    fluid_press,
    iterate,
    displace,
    velocity,
    stiffness,
    owners,
    diff_cur,
    step_cur,
    diff_past,
    step_past,
):
    high = lax.Precision.HIGHEST
    tile_count = lax.axis_size("tile")
    line_count = displace.shape[0]
    slot_count = iterate.shape[0]
    per_pair = slot_count // tile_count
    n_cur = diff_cur.shape[0]
    owner_list = owners[:, 0]
    onehot = (owner_list[:, None] == jnp.arange(tile_count, dtype=jnp.int32)[None, :]).astype(
        jnp.float32
    )
    below = (jnp.arange(line_count)[:, None] > jnp.arange(line_count)[None, :]).astype(jnp.float32)
    earlier = jnp.dot(below, onehot, precision=high)
    rank_in = jnp.sum(earlier * onehot, axis=1).astype(jnp.int32)
    slot_of = owner_list * per_pair + rank_in
    chooser = (slot_of[:, None] == jnp.arange(slot_count, dtype=jnp.int32)[None, :]).astype(
        jnp.float32
    )
    flags = jnp.sum(chooser, axis=0)
    lanes = fluid_press.shape[1]
    width = SUBSTEPS

    edge = jnp.concatenate([displace, velocity, stiffness], axis=1)
    edge_below, edge_above = halo_pair(edge, width, "tile")

    flag_rows = jnp.zeros((tile_count, 1, lanes), jnp.float32)
    flag_rows = flag_rows.at[:, 0, :per_pair].set(flags.reshape(tile_count, per_pair))
    sent = jnp.concatenate([fluid_press.reshape(tile_count, per_pair, lanes), flag_rows], axis=1)
    got = lax.all_to_all(sent, "tile", split_axis=0, concat_axis=0, tiled=True)
    returned = got[:, :per_pair, :].reshape(slot_count, lanes)
    mask = got[:, per_pair, :per_pair].reshape(slot_count)
    mask_half = mask.astype(jnp.bfloat16)

    cols = jnp.concatenate(
        [
            (diff_cur * mask_half[None, :, None]).reshape(n_cur, -1),
            (diff_past * mask_half[None, :, None]).reshape(diff_past.shape[0], -1),
        ],
        axis=0,
    )
    gram = lax.dot_general(cols, cols, (((1,), (1,)), ((), ())), preferred_element_type=jnp.float32)

    pressure = jnp.dot(chooser, returned, precision=high)
    press_below, press_above = halo_pair(pressure, width, "tile")
    packed = jnp.concatenate(
        [
            jnp.concatenate([edge_below, press_below], axis=1),
            jnp.concatenate([edge, pressure], axis=1),
            jnp.concatenate([edge_above, press_above], axis=1),
        ],
        axis=0,
    )
    field = packed[:, :lanes]
    speed = packed[:, lanes : 2 * lanes]
    stiff = packed[:, 2 * lanes : 3 * lanes]
    press = packed[:, 3 * lanes :]
    for _ in range(SUBSTEPS):
        lapl = jnp.roll(field, 1, 0) + jnp.roll(field, -1, 0) + sides(field) - 4.0 * field
        speed = speed + step_dt * (stiff * lapl + press - damping * speed)
        field = field + step_dt * speed
    field = field[width : width + line_count]
    speed = speed[width : width + line_count]

    outgoing = jnp.dot(chooser.T, field, precision=high)
    x_tilde = lax.all_to_all(outgoing, "tile", split_axis=0, concat_axis=0, tiled=True)
    resid = to_half(mask[:, None] * (x_tilde - iterate))
    inner = jnp.concatenate(
        [
            jnp.sum(diff_cur.astype(jnp.float32) * resid[None], axis=(1, 2)),
            jnp.sum(diff_past.astype(jnp.float32) * resid[None], axis=(1, 2)),
        ]
    )
    n_all = gram.shape[0]
    summed = tree_sum(jnp.concatenate([gram.reshape(-1), inner]), "tile")
    gram = summed[: n_all * n_all].reshape(n_all, n_all)
    rhs_cur = summed[n_all * n_all : n_all * n_all + n_cur]
    rhs_past = summed[n_all * n_all + n_cur :]
    cross = gram[n_cur:, :n_cur]
    inv_cur, inv_past = inverse_factors(gram[:n_cur, :n_cur], gram[n_cur:, n_cur:])
    coeff = -solve_spd(inv_cur, rhs_cur)
    projected = rhs_past + jnp.dot(cross, coeff, precision=high)
    past = solve_spd(inv_past, projected)
    coeff_half = to_half(coeff)
    past_half = to_half(past)
    upd_cur = jnp.sum(coeff_half[:, None, None] * step_cur.astype(jnp.float32), axis=0)
    upd_past = jnp.sum(past_half[:, None, None] * step_past.astype(jnp.float32), axis=0)
    update = upd_cur - upd_past
    new_iterate = mask[:, None] * (x_tilde + update)
    return (new_iterate, field, speed)


def solution(mesh):
    placed = (
        P(("runs", "tile"), None),
        P(("runs", "tile"), None),
        P(("runs", "tile"), None),
        P(("runs", "tile"), None),
        P(("runs", "tile"), None),
        P(("runs", "tile"), None),
        P(None, ("runs", "tile"), None),
        P(None, ("runs", "tile"), None),
        P(None, ("runs", "tile"), None),
        P(None, ("runs", "tile"), None),
    )
    return jax.shard_map(
        body,
        mesh=mesh,
        in_specs=placed,
        out_specs=(P(("runs", "tile"), None), P(("runs", "tile"), None), P(("runs", "tile"), None)),
        check_vma=False,
    )
```

```python
import jax
import jax.numpy as jnp
from jax import lax
from jax.experimental import pallas as pl
from jax.experimental.pallas import tpu as pltpu
from jax.sharding import PartitionSpec as P

SUBSTEPS = 4


step_dt = 1.0
damping = 0.05


def tree_parts(value, axis):
    count = lax.axis_size(axis)
    stride = 1
    while stride * 2 < count:
        value = value + lax.ppermute(value, axis, [(i, i ^ stride) for i in range(count)])
        stride *= 2
    return value, lax.ppermute(value, axis, [(i, i ^ stride) for i in range(count)])


def halo_pair(cells, width, axis):
    count = lax.axis_size(axis)
    below = lax.ppermute(cells[-width:], axis, [(i, (i + 1) % count) for i in range(count)])
    above = lax.ppermute(cells[:width], axis, [((i + 1) % count, i) for i in range(count)])
    return below, above


def to_half(value):
    return lax.reduce_precision(value, exponent_bits=8, mantissa_bits=7)


def sides(center):
    zero_col = jnp.zeros((center.shape[0], 1), jnp.float32)
    left = jnp.concatenate([zero_col, center[:, :-1]], 1)
    right = jnp.concatenate([center[:, 1:], zero_col], 1)
    return left + right


def eliminate(mats):
    state = []
    for a in mats:
        n = a.shape[0]
        rows = lax.broadcasted_iota(jnp.int32, (n, n), 0)
        cols = lax.broadcasted_iota(jnp.int32, (n, n), 1)
        state.append([a, jnp.where(rows == cols, 1.0, 0.0).astype(jnp.float32), rows, cols])
    for j in range(max(a.shape[0] for a in mats)):
        for item in state:
            a, m, rows, cols = item
            if j >= a.shape[0]:
                continue
            on_row = rows == j
            row = jnp.sum(jnp.where(on_row, a, 0.0), axis=0, keepdims=True)
            col = jnp.sum(jnp.where(cols == j, a, 0.0), axis=1, keepdims=True)
            pivot = jnp.sum(jnp.where(cols[:1] == j, row, 0.0), axis=1, keepdims=True)
            scale = 1.0 / jnp.sqrt(pivot)
            row = jnp.where(cols[:1] >= j, row * scale, 0.0)
            lower = jnp.where(rows[:, :1] > j, col * scale, 0.0)
            m_row = jnp.sum(jnp.where(on_row, m, 0.0), axis=0, keepdims=True) * scale
            item[0] = jnp.where(on_row, row, a - lower * row)
            item[1] = jnp.where(on_row, m_row, m - lower * m_row)
    return [item[1] for item in state]


def as_column(row):
    n = row.shape[1]
    eye = lax.broadcasted_iota(jnp.int32, (n, n), 0) == lax.broadcasted_iota(jnp.int32, (n, n), 1)
    return jnp.sum(jnp.where(eye, row, 0.0), axis=1, keepdims=True)


def as_row(col):
    n = col.shape[0]
    eye = lax.broadcasted_iota(jnp.int32, (n, n), 0) == lax.broadcasted_iota(jnp.int32, (n, n), 1)
    return jnp.sum(jnp.where(eye, col, 0.0), axis=0, keepdims=True)


def finish_kernel(
    own_ref, got_ref, x_ref, mask_ref, step_cur_hbm, step_past_hbm, out_ref, step_cur, step_past, sem
):
    fetch_cur = pltpu.make_async_copy(step_cur_hbm, step_cur, sem.at[0])
    fetch_past = pltpu.make_async_copy(step_past_hbm, step_past, sem.at[1])
    fetch_cur.start()
    fetch_past.start()
    n_cur = step_cur.shape[0]
    n_all = own_ref.shape[1]
    sums = own_ref[...] + got_ref[...]
    gram_cur = sums[:n_cur, :n_cur]
    gram_past = sums[n_cur:n_all, n_cur:n_all]
    cross = sums[n_cur:n_all, :n_cur]
    rhs_cur = sums[n_all:, :n_cur]
    rhs_past = sums[n_all:, n_cur:n_all]
    inv_cur, inv_past = eliminate([gram_cur, gram_past])
    inner = jnp.sum(inv_cur * rhs_cur, axis=1, keepdims=True)
    coeff = -jnp.sum(inv_cur * inner, axis=0, keepdims=True)
    projected = as_column(rhs_past) + jnp.sum(cross * coeff, axis=1, keepdims=True)
    inner = jnp.sum(inv_past * as_row(projected), axis=1, keepdims=True)
    past = jnp.sum(inv_past * inner, axis=0, keepdims=True)
    coeff = coeff.astype(jnp.bfloat16).astype(jnp.float32)
    past = past.astype(jnp.bfloat16).astype(jnp.float32)
    fetch_cur.wait()
    fetch_past.wait()

    def weighted(weights, planes):
        lanes = lax.broadcasted_iota(jnp.int32, weights.shape, 1)

        def add(c, acc):
            weight = jnp.sum(jnp.where(lanes == c, weights, 0.0), axis=1, keepdims=True)
            return acc + weight * planes[c].astype(jnp.float32)

        return lax.fori_loop(0, planes.shape[0], add, jnp.zeros(out_ref.shape, jnp.float32))

    update = weighted(coeff, step_cur) - weighted(past, step_past)
    out_ref[...] = mask_ref[...] * (x_ref[...] + update)


def finish(own, got, x_tilde, mask, step_cur, step_past):
    vmem = pl.BlockSpec(memory_space=pltpu.VMEM)
    hbm = pl.BlockSpec(memory_space=pl.ANY)
    return pl.pallas_call(
        finish_kernel,
        out_shape=jax.ShapeDtypeStruct(x_tilde.shape, jnp.float32),
        in_specs=[vmem, vmem, vmem, vmem, hbm, hbm],
        out_specs=vmem,
        scratch_shapes=[
            pltpu.VMEM(step_cur.shape, step_cur.dtype),
            pltpu.VMEM(step_past.shape, step_past.dtype),
            pltpu.SemaphoreType.DMA((2,)),
        ],
    )(own, got, x_tilde, mask, step_cur, step_past)


def body(
    fluid_press,
    iterate,
    displace,
    velocity,
    stiffness,
    owners,
    diff_cur,
    step_cur,
    diff_past,
    step_past,
):
    high = lax.Precision.HIGHEST
    tile_count = lax.axis_size("tile")
    line_count = displace.shape[0]
    slot_count = iterate.shape[0]
    per_pair = slot_count // tile_count
    n_cur = diff_cur.shape[0]
    owner_list = owners[:, 0]
    onehot = (owner_list[:, None] == jnp.arange(tile_count, dtype=jnp.int32)[None, :]).astype(
        jnp.float32
    )
    below = (jnp.arange(line_count)[:, None] > jnp.arange(line_count)[None, :]).astype(jnp.float32)
    earlier = jnp.dot(below, onehot, precision=high)
    rank_in = jnp.sum(earlier * onehot, axis=1).astype(jnp.int32)
    slot_of = owner_list * per_pair + rank_in
    chooser = (slot_of[:, None] == jnp.arange(slot_count, dtype=jnp.int32)[None, :]).astype(
        jnp.float32
    )
    flags = jnp.sum(chooser, axis=0)
    lanes = fluid_press.shape[1]
    width = SUBSTEPS

    edge = jnp.concatenate([displace, velocity, stiffness], axis=1)
    edge_below, edge_above = halo_pair(edge, width, "tile")

    flag_rows = jnp.zeros((tile_count, 1, lanes), jnp.float32)
    flag_rows = flag_rows.at[:, 0, :per_pair].set(flags.reshape(tile_count, per_pair))
    sent = jnp.concatenate([fluid_press.reshape(tile_count, per_pair, lanes), flag_rows], axis=1)
    got = lax.all_to_all(sent, "tile", split_axis=0, concat_axis=0, tiled=True)
    returned = got[:, :per_pair, :].reshape(slot_count, lanes)
    mask = got[:, per_pair, :per_pair].reshape(slot_count)
    mask_half = mask.astype(jnp.bfloat16)

    cols = jnp.concatenate(
        [
            (diff_cur * mask_half[None, :, None]).reshape(n_cur, -1),
            (diff_past * mask_half[None, :, None]).reshape(diff_past.shape[0], -1),
        ],
        axis=0,
    )
    gram = lax.dot_general(cols, cols, (((1,), (1,)), ((), ())), preferred_element_type=jnp.float32)

    pressure = jnp.dot(chooser, returned, precision=high)
    press_below, press_above = halo_pair(pressure, width, "tile")
    packed = jnp.concatenate(
        [
            jnp.concatenate([edge_below, press_below], axis=1),
            jnp.concatenate([edge, pressure], axis=1),
            jnp.concatenate([edge_above, press_above], axis=1),
        ],
        axis=0,
    )
    field = packed[:, :lanes]
    speed = packed[:, lanes : 2 * lanes]
    stiff = packed[:, 2 * lanes : 3 * lanes]
    press = packed[:, 3 * lanes :]
    for _ in range(SUBSTEPS):
        lapl = jnp.roll(field, 1, 0) + jnp.roll(field, -1, 0) + sides(field) - 4.0 * field
        speed = speed + step_dt * (stiff * lapl + press - damping * speed)
        field = field + step_dt * speed
    field = field[width : width + line_count]
    speed = speed[width : width + line_count]

    outgoing = jnp.dot(chooser.T, field, precision=high)
    x_tilde = lax.all_to_all(outgoing, "tile", split_axis=0, concat_axis=0, tiled=True)
    resid = to_half(mask[:, None] * (x_tilde - iterate))
    inner = jnp.concatenate(
        [
            jnp.sum(diff_cur.astype(jnp.float32) * resid[None], axis=(1, 2)),
            jnp.sum(diff_past.astype(jnp.float32) * resid[None], axis=(1, 2)),
        ]
    )
    own, got = tree_parts(jnp.concatenate([gram, inner[None]], axis=0), "tile")
    new_iterate = finish(own, got, x_tilde, mask[:, None], step_cur, step_past)
    return (new_iterate, field, speed)


def solution(mesh):
    placed = (
        P(("runs", "tile"), None),
        P(("runs", "tile"), None),
        P(("runs", "tile"), None),
        P(("runs", "tile"), None),
        P(("runs", "tile"), None),
        P(("runs", "tile"), None),
        P(None, ("runs", "tile"), None),
        P(None, ("runs", "tile"), None),
        P(None, ("runs", "tile"), None),
        P(None, ("runs", "tile"), None),
    )
    return jax.shard_map(
        body,
        mesh=mesh,
        in_specs=placed,
        out_specs=(P(("runs", "tile"), None), P(("runs", "tile"), None), P(("runs", "tile"), None)),
        check_vma=False,
    )
```

```python
import jax
import jax.numpy as jnp
from jax import lax
from jax.experimental import pallas as pl
from jax.sharding import PartitionSpec as P

SUBSTEPS = 4


step_dt = 1.0
damping = 0.05


def tree_parts(value, axis):
    count = lax.axis_size(axis)
    stride = 1
    while stride * 2 < count:
        value = value + lax.ppermute(value, axis, [(i, i ^ stride) for i in range(count)])
        stride *= 2
    return value, lax.ppermute(value, axis, [(i, i ^ stride) for i in range(count)])


def halo_pair(cells, width, axis):
    count = lax.axis_size(axis)
    below = lax.ppermute(cells[-width:], axis, [(i, (i + 1) % count) for i in range(count)])
    above = lax.ppermute(cells[:width], axis, [((i + 1) % count, i) for i in range(count)])
    return below, above


def to_half(value):
    return lax.reduce_precision(value, exponent_bits=8, mantissa_bits=7)


def sides(center):
    zero_col = jnp.zeros((center.shape[0], 1), jnp.float32)
    left = jnp.concatenate([zero_col, center[:, :-1]], 1)
    right = jnp.concatenate([center[:, 1:], zero_col], 1)
    return left + right


def eliminate(mats):
    state = []
    for a in mats:
        n = a.shape[0]
        rows = lax.broadcasted_iota(jnp.int32, (n, n), 0)
        cols = lax.broadcasted_iota(jnp.int32, (n, n), 1)
        state.append([a, jnp.where(rows == cols, 1.0, 0.0).astype(jnp.float32), rows, cols])
    for j in range(max(a.shape[0] for a in mats)):
        for item in state:
            a, m, rows, cols = item
            if j >= a.shape[0]:
                continue
            on_row = rows == j
            row = jnp.sum(jnp.where(on_row, a, 0.0), axis=0, keepdims=True)
            col = jnp.sum(jnp.where(cols == j, a, 0.0), axis=1, keepdims=True)
            pivot = jnp.sum(jnp.where(cols[:1] == j, row, 0.0), axis=1, keepdims=True)
            scale = 1.0 / jnp.sqrt(pivot)
            row = jnp.where(cols[:1] >= j, row * scale, 0.0)
            lower = jnp.where(rows[:, :1] > j, col * scale, 0.0)
            m_row = jnp.sum(jnp.where(on_row, m, 0.0), axis=0, keepdims=True) * scale
            item[0] = jnp.where(on_row, row, a - lower * row)
            item[1] = jnp.where(on_row, m_row, m - lower * m_row)
    return [item[1] for item in state]


def as_column(row):
    n = row.shape[1]
    eye = lax.broadcasted_iota(jnp.int32, (n, n), 0) == lax.broadcasted_iota(jnp.int32, (n, n), 1)
    return jnp.sum(jnp.where(eye, row, 0.0), axis=1, keepdims=True)


def as_row(col):
    n = col.shape[0]
    eye = lax.broadcasted_iota(jnp.int32, (n, n), 0) == lax.broadcasted_iota(jnp.int32, (n, n), 1)
    return jnp.sum(jnp.where(eye, col, 0.0), axis=0, keepdims=True)


def solve_kernel(own_ref, got_ref, coeff_ref, past_ref):
    n_cur = coeff_ref.shape[1]
    n_all = own_ref.shape[1]
    sums = own_ref[...] + got_ref[...]
    gram_cur = sums[:n_cur, :n_cur]
    gram_past = sums[n_cur:n_all, n_cur:n_all]
    cross = sums[n_cur:n_all, :n_cur]
    rhs_cur = sums[n_all:, :n_cur]
    rhs_past = sums[n_all:, n_cur:n_all]
    inv_cur, inv_past = eliminate([gram_cur, gram_past])
    inner = jnp.sum(inv_cur * rhs_cur, axis=1, keepdims=True)
    coeff = -jnp.sum(inv_cur * inner, axis=0, keepdims=True)
    projected = as_column(rhs_past) + jnp.sum(cross * coeff, axis=1, keepdims=True)
    inner = jnp.sum(inv_past * as_row(projected), axis=1, keepdims=True)
    past = jnp.sum(inv_past * inner, axis=0, keepdims=True)
    coeff_ref[...] = coeff.astype(jnp.bfloat16).astype(jnp.float32)
    past_ref[...] = past.astype(jnp.bfloat16).astype(jnp.float32)


def solve_both(own, got, n_cur):
    n_past = own.shape[1] - n_cur
    shapes = (jax.ShapeDtypeStruct((1, n_cur), jnp.float32), jax.ShapeDtypeStruct((1, n_past), jnp.float32))
    coeff, past = pl.pallas_call(solve_kernel, out_shape=shapes)(own, got)
    return coeff[0], past[0]


def body(
    fluid_press,
    iterate,
    displace,
    velocity,
    stiffness,
    owners,
    diff_cur,
    step_cur,
    diff_past,
    step_past,
):
    high = lax.Precision.HIGHEST
    tile_count = lax.axis_size("tile")
    line_count = displace.shape[0]
    slot_count = iterate.shape[0]
    per_pair = slot_count // tile_count
    n_cur = diff_cur.shape[0]
    owner_list = owners[:, 0]
    onehot = (owner_list[:, None] == jnp.arange(tile_count, dtype=jnp.int32)[None, :]).astype(
        jnp.float32
    )
    below = (jnp.arange(line_count)[:, None] > jnp.arange(line_count)[None, :]).astype(jnp.float32)
    earlier = jnp.dot(below, onehot, precision=high)
    rank_in = jnp.sum(earlier * onehot, axis=1).astype(jnp.int32)
    slot_of = owner_list * per_pair + rank_in
    chooser = (slot_of[:, None] == jnp.arange(slot_count, dtype=jnp.int32)[None, :]).astype(
        jnp.float32
    )
    flags = jnp.sum(chooser, axis=0)
    lanes = fluid_press.shape[1]
    width = SUBSTEPS

    edge = jnp.concatenate([displace, velocity, stiffness], axis=1)
    edge_below, edge_above = halo_pair(edge, width, "tile")

    flag_rows = jnp.zeros((tile_count, 1, lanes), jnp.float32)
    flag_rows = flag_rows.at[:, 0, :per_pair].set(flags.reshape(tile_count, per_pair))
    sent = jnp.concatenate([fluid_press.reshape(tile_count, per_pair, lanes), flag_rows], axis=1)
    got = lax.all_to_all(sent, "tile", split_axis=0, concat_axis=0, tiled=True)
    returned = got[:, :per_pair, :].reshape(slot_count, lanes)
    mask = got[:, per_pair, :per_pair].reshape(slot_count)
    mask_half = mask.astype(jnp.bfloat16)

    cols = jnp.concatenate(
        [
            (diff_cur * mask_half[None, :, None]).reshape(n_cur, -1),
            (diff_past * mask_half[None, :, None]).reshape(diff_past.shape[0], -1),
        ],
        axis=0,
    )
    gram = lax.dot_general(cols, cols, (((1,), (1,)), ((), ())), preferred_element_type=jnp.float32)

    pressure = jnp.dot(chooser, returned, precision=high)
    press_below, press_above = halo_pair(pressure, width, "tile")
    packed = jnp.concatenate(
        [
            jnp.concatenate([edge_below, press_below], axis=1),
            jnp.concatenate([edge, pressure], axis=1),
            jnp.concatenate([edge_above, press_above], axis=1),
        ],
        axis=0,
    )
    field = packed[:, :lanes]
    speed = packed[:, lanes : 2 * lanes]
    stiff = packed[:, 2 * lanes : 3 * lanes]
    press = packed[:, 3 * lanes :]
    for _ in range(SUBSTEPS):
        lapl = jnp.roll(field, 1, 0) + jnp.roll(field, -1, 0) + sides(field) - 4.0 * field
        speed = speed + step_dt * (stiff * lapl + press - damping * speed)
        field = field + step_dt * speed
    field = field[width : width + line_count]
    speed = speed[width : width + line_count]

    outgoing = jnp.dot(chooser.T, field, precision=high)
    x_tilde = lax.all_to_all(outgoing, "tile", split_axis=0, concat_axis=0, tiled=True)
    resid = to_half(mask[:, None] * (x_tilde - iterate))
    inner = jnp.concatenate(
        [
            jnp.sum(diff_cur.astype(jnp.float32) * resid[None], axis=(1, 2)),
            jnp.sum(diff_past.astype(jnp.float32) * resid[None], axis=(1, 2)),
        ]
    )
    own, got = tree_parts(jnp.concatenate([gram, inner[None]], axis=0), "tile")
    coeff_half, past_half = solve_both(own, got, n_cur)
    upd_cur = jnp.sum(coeff_half[:, None, None] * step_cur.astype(jnp.float32), axis=0)
    upd_past = jnp.sum(past_half[:, None, None] * step_past.astype(jnp.float32), axis=0)
    update = upd_cur - upd_past
    new_iterate = mask[:, None] * (x_tilde + update)
    return (new_iterate, field, speed)


def solution(mesh):
    placed = (
        P(("runs", "tile"), None),
        P(("runs", "tile"), None),
        P(("runs", "tile"), None),
        P(("runs", "tile"), None),
        P(("runs", "tile"), None),
        P(("runs", "tile"), None),
        P(None, ("runs", "tile"), None),
        P(None, ("runs", "tile"), None),
        P(None, ("runs", "tile"), None),
        P(None, ("runs", "tile"), None),
    )
    return jax.shard_map(
        body,
        mesh=mesh,
        in_specs=placed,
        out_specs=(P(("runs", "tile"), None), P(("runs", "tile"), None), P(("runs", "tile"), None)),
        check_vma=False,
    )
```

```python
import jax
import jax.numpy as jnp
from jax import lax
from jax.experimental import pallas as pl
from jax.sharding import PartitionSpec as P


SUBSTEPS = 4


step_dt = 1.0
damping = 0.05


def tree_sum(value, axis):
    count = lax.axis_size(axis)
    if count & (count - 1):
        return lax.psum(value, axis)
    stride = 1
    while stride < count:
        value = value + lax.ppermute(value, axis, [(i, i ^ stride) for i in range(count)])
        stride *= 2
    return value


def halo_pair(cells, width, axis):
    count = lax.axis_size(axis)
    below = lax.ppermute(cells[-width:], axis, [(i, (i + 1) % count) for i in range(count)])
    above = lax.ppermute(cells[:width], axis, [((i + 1) % count, i) for i in range(count)])
    return below, above


def to_half(value):
    return lax.reduce_precision(value, exponent_bits=8, mantissa_bits=7)


def sides(center):
    zero_col = jnp.zeros((center.shape[0], 1), jnp.float32)
    left = jnp.concatenate([zero_col, center[:, :-1]], 1)
    right = jnp.concatenate([center[:, 1:], zero_col], 1)
    return left + right


def eliminate(mats):
    state = []
    for a in mats:
        n = a.shape[0]
        rows = lax.broadcasted_iota(jnp.int32, (n, n), 0)
        cols = lax.broadcasted_iota(jnp.int32, (n, n), 1)
        state.append([a, jnp.where(rows == cols, 1.0, 0.0).astype(jnp.float32), rows, cols])
    for j in range(max(a.shape[0] for a in mats)):
        for item in state:
            a, m, rows, cols = item
            if j >= a.shape[0]:
                continue
            on_row = rows == j
            row = jnp.sum(jnp.where(on_row, a, 0.0), axis=0, keepdims=True)
            col = jnp.sum(jnp.where(cols == j, a, 0.0), axis=1, keepdims=True)
            pivot = jnp.sum(jnp.where(cols[:1] == j, row, 0.0), axis=1, keepdims=True)
            scale = 1.0 / jnp.sqrt(pivot)
            row = jnp.where(cols[:1] >= j, row * scale, 0.0)
            lower = jnp.where(rows[:, :1] > j, col * scale, 0.0)
            m_row = jnp.sum(jnp.where(on_row, m, 0.0), axis=0, keepdims=True) * scale
            item[0] = jnp.where(on_row, row, a - lower * row)
            item[1] = jnp.where(on_row, m_row, m - lower * m_row)
    return [item[1] for item in state]


def as_column(row):
    n = row.shape[1]
    eye = lax.broadcasted_iota(jnp.int32, (n, n), 0) == lax.broadcasted_iota(jnp.int32, (n, n), 1)
    return jnp.sum(jnp.where(eye, row, 0.0), axis=1, keepdims=True)


def as_row(col):
    n = col.shape[0]
    eye = lax.broadcasted_iota(jnp.int32, (n, n), 0) == lax.broadcasted_iota(jnp.int32, (n, n), 1)
    return jnp.sum(jnp.where(eye, col, 0.0), axis=0, keepdims=True)


def solve_kernel(sums_ref, coeff_ref, past_ref):
    n_cur = coeff_ref.shape[1]
    n_all = sums_ref.shape[1]
    sums = sums_ref[...]
    gram_cur = sums[:n_cur, :n_cur]
    gram_past = sums[n_cur:n_all, n_cur:n_all]
    cross = sums[n_cur:n_all, :n_cur]
    rhs_cur = sums[n_all:, :n_cur]
    rhs_past = sums[n_all:, n_cur:n_all]
    inv_cur, inv_past = eliminate([gram_cur, gram_past])
    inner = jnp.sum(inv_cur * rhs_cur, axis=1, keepdims=True)
    coeff = -jnp.sum(inv_cur * inner, axis=0, keepdims=True)
    projected = as_column(rhs_past) + jnp.sum(cross * coeff, axis=1, keepdims=True)
    inner = jnp.sum(inv_past * as_row(projected), axis=1, keepdims=True)
    coeff_ref[...] = coeff
    past_ref[...] = jnp.sum(inv_past * inner, axis=0, keepdims=True)


def solve_both(sums, n_cur):
    n_past = sums.shape[1] - n_cur
    shapes = (jax.ShapeDtypeStruct((1, n_cur), jnp.float32), jax.ShapeDtypeStruct((1, n_past), jnp.float32))
    coeff, past = pl.pallas_call(solve_kernel, out_shape=shapes)(sums)
    return coeff[0], past[0]


def body(
    fluid_press,
    iterate,
    displace,
    velocity,
    stiffness,
    owners,
    diff_cur,
    step_cur,
    diff_past,
    step_past,
):
    high = lax.Precision.HIGHEST
    tile_count = lax.axis_size("tile")
    line_count = displace.shape[0]
    slot_count = iterate.shape[0]
    per_pair = slot_count // tile_count
    n_cur = diff_cur.shape[0]
    owner_list = owners[:, 0]
    onehot = (owner_list[:, None] == jnp.arange(tile_count, dtype=jnp.int32)[None, :]).astype(
        jnp.float32
    )
    below = (jnp.arange(line_count)[:, None] > jnp.arange(line_count)[None, :]).astype(jnp.float32)
    earlier = jnp.dot(below, onehot, precision=high)
    rank_in = jnp.sum(earlier * onehot, axis=1).astype(jnp.int32)
    slot_of = owner_list * per_pair + rank_in
    chooser = (slot_of[:, None] == jnp.arange(slot_count, dtype=jnp.int32)[None, :]).astype(
        jnp.float32
    )
    flags = jnp.sum(chooser, axis=0)
    lanes = fluid_press.shape[1]
    width = SUBSTEPS

    edge = jnp.concatenate([displace, velocity, stiffness], axis=1)
    edge_below, edge_above = halo_pair(edge, width, "tile")

    flag_rows = jnp.zeros((tile_count, 1, lanes), jnp.float32)
    flag_rows = flag_rows.at[:, 0, :per_pair].set(flags.reshape(tile_count, per_pair))
    sent = jnp.concatenate([fluid_press.reshape(tile_count, per_pair, lanes), flag_rows], axis=1)
    got = lax.all_to_all(sent, "tile", split_axis=0, concat_axis=0, tiled=True)
    returned = got[:, :per_pair, :].reshape(slot_count, lanes)
    mask = got[:, per_pair, :per_pair].reshape(slot_count)
    mask_half = mask.astype(jnp.bfloat16)

    cols = jnp.concatenate(
        [
            (diff_cur * mask_half[None, :, None]).reshape(n_cur, -1),
            (diff_past * mask_half[None, :, None]).reshape(diff_past.shape[0], -1),
        ],
        axis=0,
    )
    gram = lax.dot_general(cols, cols, (((1,), (1,)), ((), ())), preferred_element_type=jnp.float32)

    pressure = jnp.dot(chooser, returned, precision=high)
    press_below, press_above = halo_pair(pressure, width, "tile")
    packed = jnp.concatenate(
        [
            jnp.concatenate([edge_below, press_below], axis=1),
            jnp.concatenate([edge, pressure], axis=1),
            jnp.concatenate([edge_above, press_above], axis=1),
        ],
        axis=0,
    )
    field = packed[:, :lanes]
    speed = packed[:, lanes : 2 * lanes]
    stiff = packed[:, 2 * lanes : 3 * lanes]
    press = packed[:, 3 * lanes :]
    for _ in range(SUBSTEPS):
        lapl = jnp.roll(field, 1, 0) + jnp.roll(field, -1, 0) + sides(field) - 4.0 * field
        speed = speed + step_dt * (stiff * lapl + press - damping * speed)
        field = field + step_dt * speed
    field = field[width : width + line_count]
    speed = speed[width : width + line_count]

    outgoing = jnp.dot(chooser.T, field, precision=high)
    x_tilde = lax.all_to_all(outgoing, "tile", split_axis=0, concat_axis=0, tiled=True)
    resid = to_half(mask[:, None] * (x_tilde - iterate))
    inner = jnp.concatenate(
        [
            jnp.sum(diff_cur.astype(jnp.float32) * resid[None], axis=(1, 2)),
            jnp.sum(diff_past.astype(jnp.float32) * resid[None], axis=(1, 2)),
        ]
    )
    summed = tree_sum(jnp.concatenate([gram, inner[None]], axis=0), "tile")
    coeff, past = solve_both(summed, n_cur)
    coeff_half = to_half(coeff)
    past_half = to_half(past)
    upd_cur = jnp.sum(coeff_half[:, None, None] * step_cur.astype(jnp.float32), axis=0)
    upd_past = jnp.sum(past_half[:, None, None] * step_past.astype(jnp.float32), axis=0)
    update = upd_cur - upd_past
    new_iterate = mask[:, None] * (x_tilde + update)
    return (new_iterate, field, speed)


def solution(mesh):
    placed = (
        P(("runs", "tile"), None),
        P(("runs", "tile"), None),
        P(("runs", "tile"), None),
        P(("runs", "tile"), None),
        P(("runs", "tile"), None),
        P(("runs", "tile"), None),
        P(None, ("runs", "tile"), None),
        P(None, ("runs", "tile"), None),
        P(None, ("runs", "tile"), None),
        P(None, ("runs", "tile"), None),
    )
    return jax.shard_map(
        body,
        mesh=mesh,
        in_specs=placed,
        out_specs=(P(("runs", "tile"), None), P(("runs", "tile"), None), P(("runs", "tile"), None)),
        check_vma=False,
    )
```

```python
import jax
import jax.numpy as jnp
from jax import lax
from jax.experimental import pallas as pl
from jax.sharding import PartitionSpec as P


SUBSTEPS = 4


step_dt = 1.0
damping = 0.05


def tree_sum(value, axis):
    count = lax.axis_size(axis)
    if count & (count - 1):
        return lax.psum(value, axis)
    stride = 1
    while stride < count:
        value = value + lax.ppermute(value, axis, [(i, i ^ stride) for i in range(count)])
        stride *= 2
    return value


def halo_pair(cells, width, axis):
    count = lax.axis_size(axis)
    below = lax.ppermute(cells[-width:], axis, [(i, (i + 1) % count) for i in range(count)])
    above = lax.ppermute(cells[:width], axis, [((i + 1) % count, i) for i in range(count)])
    return below, above


def to_half(value):
    return lax.reduce_precision(value, exponent_bits=8, mantissa_bits=7)


def sides(center):
    zero_col = jnp.zeros((center.shape[0], 1), jnp.float32)
    left = jnp.concatenate([zero_col, center[:, :-1]], 1)
    right = jnp.concatenate([center[:, 1:], zero_col], 1)
    return left + right


def eliminate(mats):
    state = []
    for a in mats:
        n = a.shape[0]
        rows = lax.broadcasted_iota(jnp.int32, (n, n), 0)
        cols = lax.broadcasted_iota(jnp.int32, (n, n), 1)
        state.append([a, jnp.where(rows == cols, 1.0, 0.0).astype(jnp.float32), rows, cols])
    for j in range(max(a.shape[0] for a in mats)):
        for item in state:
            a, m, rows, cols = item
            if j >= a.shape[0]:
                continue
            on_row = rows == j
            row = jnp.sum(jnp.where(on_row, a, 0.0), axis=0, keepdims=True)
            col = jnp.sum(jnp.where(cols == j, a, 0.0), axis=1, keepdims=True)
            pivot = jnp.sum(jnp.where(cols[:1] == j, row, 0.0), axis=1, keepdims=True)
            scale = 1.0 / jnp.sqrt(pivot)
            row = jnp.where(cols[:1] >= j, row * scale, 0.0)
            lower = jnp.where(rows[:, :1] > j, col * scale, 0.0)
            m_row = jnp.sum(jnp.where(on_row, m, 0.0), axis=0, keepdims=True) * scale
            item[0] = jnp.where(on_row, row, a - lower * row)
            item[1] = jnp.where(on_row, m_row, m - lower * m_row)
    return [item[1] for item in state]


def as_column(row):
    n = row.shape[1]
    eye = lax.broadcasted_iota(jnp.int32, (n, n), 0) == lax.broadcasted_iota(jnp.int32, (n, n), 1)
    return jnp.sum(jnp.where(eye, row, 0.0), axis=1, keepdims=True)


def as_row(col):
    n = col.shape[0]
    eye = lax.broadcasted_iota(jnp.int32, (n, n), 0) == lax.broadcasted_iota(jnp.int32, (n, n), 1)
    return jnp.sum(jnp.where(eye, col, 0.0), axis=0, keepdims=True)


def solve_kernel(sums_ref, coeff_ref, past_ref):
    n_cur = coeff_ref.shape[1]
    n_all = sums_ref.shape[1]
    sums = sums_ref[...]
    gram_cur = sums[:n_cur, :n_cur]
    gram_past = sums[n_cur:n_all, n_cur:n_all]
    cross = sums[n_cur:n_all, :n_cur]
    rhs_cur = sums[n_all:, :n_cur]
    rhs_past = sums[n_all:, n_cur:n_all]
    inv_cur, inv_past = eliminate([gram_cur, gram_past])
    inner = jnp.sum(inv_cur * rhs_cur, axis=1, keepdims=True)
    coeff = -jnp.sum(inv_cur * inner, axis=0, keepdims=True)
    projected = as_column(rhs_past) + jnp.sum(cross * coeff, axis=1, keepdims=True)
    inner = jnp.sum(inv_past * as_row(projected), axis=1, keepdims=True)
    coeff_ref[...] = coeff
    past_ref[...] = jnp.sum(inv_past * inner, axis=0, keepdims=True)


def solve_both(sums, n_cur):
    n_past = sums.shape[1] - n_cur
    shapes = (jax.ShapeDtypeStruct((1, n_cur), jnp.float32), jax.ShapeDtypeStruct((1, n_past), jnp.float32))
    coeff, past = pl.pallas_call(solve_kernel, out_shape=shapes)(sums)
    return coeff[0], past[0]


def body(
    fluid_press,
    iterate,
    displace,
    velocity,
    stiffness,
    owners,
    diff_cur,
    step_cur,
    diff_past,
    step_past,
):
    high = lax.Precision.HIGHEST
    tile_count = lax.axis_size("tile")
    line_count = displace.shape[0]
    slot_count = iterate.shape[0]
    per_pair = slot_count // tile_count
    n_cur = diff_cur.shape[0]
    owner_list = owners[:, 0]
    onehot = (owner_list[:, None] == jnp.arange(tile_count, dtype=jnp.int32)[None, :]).astype(
        jnp.float32
    )
    below = (jnp.arange(line_count)[:, None] > jnp.arange(line_count)[None, :]).astype(jnp.float32)
    earlier = jnp.dot(below, onehot, precision=high)
    rank_in = jnp.sum(earlier * onehot, axis=1).astype(jnp.int32)
    slot_of = owner_list * per_pair + rank_in
    chooser = (slot_of[:, None] == jnp.arange(slot_count, dtype=jnp.int32)[None, :]).astype(
        jnp.float32
    )
    counts = jnp.sum(onehot, axis=0)
    flags = (jnp.arange(per_pair, dtype=jnp.float32)[None, :] < counts[:, None]).astype(jnp.float32)
    lanes = fluid_press.shape[1]
    width = SUBSTEPS

    edge = jnp.concatenate([displace, velocity, stiffness], axis=1)
    edge_below, edge_above = halo_pair(edge, width, "tile")

    flag_count = 8 - per_pair % 8
    flag_rows = jnp.zeros((tile_count, flag_count, lanes), jnp.float32)
    flag_rows = flag_rows.at[:, 0, :per_pair].set(flags)
    sent = jnp.concatenate([fluid_press.reshape(tile_count, per_pair, lanes), flag_rows], axis=1)
    got = lax.all_to_all(sent, "tile", split_axis=0, concat_axis=0, tiled=True)
    returned = got[:, :per_pair, :].reshape(slot_count, lanes)
    mask = got[:, per_pair, :per_pair].reshape(slot_count)
    mask_half = mask.astype(jnp.bfloat16)

    cols = jnp.concatenate(
        [
            (diff_cur * mask_half[None, :, None]).reshape(n_cur, -1),
            (diff_past * mask_half[None, :, None]).reshape(diff_past.shape[0], -1),
        ],
        axis=0,
    )
    gram = lax.dot_general(cols, cols, (((1,), (1,)), ((), ())), preferred_element_type=jnp.float32)

    pressure = jnp.dot(chooser, returned, precision=high)
    press_below, press_above = halo_pair(pressure, width, "tile")
    packed = jnp.concatenate(
        [
            jnp.concatenate([edge_below, press_below], axis=1),
            jnp.concatenate([edge, pressure], axis=1),
            jnp.concatenate([edge_above, press_above], axis=1),
        ],
        axis=0,
    )
    field = packed[:, :lanes]
    speed = packed[:, lanes : 2 * lanes]
    stiff = packed[:, 2 * lanes : 3 * lanes]
    press = packed[:, 3 * lanes :]
    for _ in range(SUBSTEPS):
        lapl = jnp.roll(field, 1, 0) + jnp.roll(field, -1, 0) + sides(field) - 4.0 * field
        speed = speed + step_dt * (stiff * lapl + press - damping * speed)
        field = field + step_dt * speed
    field = field[width : width + line_count]
    speed = speed[width : width + line_count]

    outgoing = jnp.dot(chooser.T, field, precision=high)
    x_tilde = lax.all_to_all(outgoing, "tile", split_axis=0, concat_axis=0, tiled=True)
    resid = to_half(mask[:, None] * (x_tilde - iterate))
    inner = jnp.concatenate(
        [
            jnp.sum(diff_cur.astype(jnp.float32) * resid[None], axis=(1, 2)),
            jnp.sum(diff_past.astype(jnp.float32) * resid[None], axis=(1, 2)),
        ]
    )
    summed = tree_sum(jnp.concatenate([gram, inner[None]], axis=0), "tile")
    coeff, past = solve_both(summed, n_cur)
    coeff_half = to_half(coeff)
    past_half = to_half(past)
    upd_cur = jnp.sum(coeff_half[:, None, None] * step_cur.astype(jnp.float32), axis=0)
    upd_past = jnp.sum(past_half[:, None, None] * step_past.astype(jnp.float32), axis=0)
    update = upd_cur - upd_past
    new_iterate = mask[:, None] * (x_tilde + update)
    return (new_iterate, field, speed)


def solution(mesh):
    placed = (
        P(("runs", "tile"), None),
        P(("runs", "tile"), None),
        P(("runs", "tile"), None),
        P(("runs", "tile"), None),
        P(("runs", "tile"), None),
        P(("runs", "tile"), None),
        P(None, ("runs", "tile"), None),
        P(None, ("runs", "tile"), None),
        P(None, ("runs", "tile"), None),
        P(None, ("runs", "tile"), None),
    )
    return jax.shard_map(
        body,
        mesh=mesh,
        in_specs=placed,
        out_specs=(P(("runs", "tile"), None), P(("runs", "tile"), None), P(("runs", "tile"), None)),
        check_vma=False,
    )
```

```python
import jax
import jax.numpy as jnp
from jax import lax
from jax.experimental import pallas as pl
from jax.sharding import PartitionSpec as P


SUBSTEPS = 4


step_dt = 1.0
damping = 0.05


def tree_sum(value, axis):
    count = lax.axis_size(axis)
    if count & (count - 1):
        return lax.psum(value, axis)
    stride = 1
    while stride < count:
        value = value + lax.ppermute(value, axis, [(i, i ^ stride) for i in range(count)])
        stride *= 2
    return value


def halo_pair(cells, width, axis):
    count = lax.axis_size(axis)
    below = lax.ppermute(cells[-width:], axis, [(i, (i + 1) % count) for i in range(count)])
    above = lax.ppermute(cells[:width], axis, [((i + 1) % count, i) for i in range(count)])
    return below, above


def to_half(value):
    return lax.reduce_precision(value, exponent_bits=8, mantissa_bits=7)


def sides(center):
    zero_col = jnp.zeros((center.shape[0], 1), jnp.float32)
    left = jnp.concatenate([zero_col, center[:, :-1]], 1)
    right = jnp.concatenate([center[:, 1:], zero_col], 1)
    return left + right


def eliminate(mats):
    state = []
    for a in mats:
        n = a.shape[0]
        rows = lax.broadcasted_iota(jnp.int32, (n, n), 0)
        cols = lax.broadcasted_iota(jnp.int32, (n, n), 1)
        state.append([a, jnp.where(rows == cols, 1.0, 0.0).astype(jnp.float32), rows, cols])
    for j in range(max(a.shape[0] for a in mats)):
        for item in state:
            a, m, rows, cols = item
            if j >= a.shape[0]:
                continue
            on_row = rows == j
            row = jnp.sum(jnp.where(on_row, a, 0.0), axis=0, keepdims=True)
            col = jnp.sum(jnp.where(cols == j, a, 0.0), axis=1, keepdims=True)
            pivot = jnp.sum(jnp.where(cols[:1] == j, row, 0.0), axis=1, keepdims=True)
            scale = 1.0 / jnp.sqrt(pivot)
            row = jnp.where(cols[:1] >= j, row * scale, 0.0)
            lower = jnp.where(rows[:, :1] > j, col * scale, 0.0)
            m_row = jnp.sum(jnp.where(on_row, m, 0.0), axis=0, keepdims=True) * scale
            item[0] = jnp.where(on_row, row, a - lower * row)
            item[1] = jnp.where(on_row, m_row, m - lower * m_row)
    return [item[1] for item in state]


def as_column(row):
    n = row.shape[1]
    eye = lax.broadcasted_iota(jnp.int32, (n, n), 0) == lax.broadcasted_iota(jnp.int32, (n, n), 1)
    return jnp.sum(jnp.where(eye, row, 0.0), axis=1, keepdims=True)


def as_row(col):
    n = col.shape[0]
    eye = lax.broadcasted_iota(jnp.int32, (n, n), 0) == lax.broadcasted_iota(jnp.int32, (n, n), 1)
    return jnp.sum(jnp.where(eye, col, 0.0), axis=0, keepdims=True)


def solve_kernel(sums_ref, coeff_ref, past_ref):
    n_cur = coeff_ref.shape[1]
    n_all = sums_ref.shape[1]
    sums = sums_ref[...]
    gram_cur = sums[:n_cur, :n_cur]
    gram_past = sums[n_cur:n_all, n_cur:n_all]
    cross = sums[n_cur:n_all, :n_cur]
    rhs_cur = sums[n_all:, :n_cur]
    rhs_past = sums[n_all:, n_cur:n_all]
    inv_cur, inv_past = eliminate([gram_cur, gram_past])
    inner = jnp.sum(inv_cur * rhs_cur, axis=1, keepdims=True)
    coeff = -jnp.sum(inv_cur * inner, axis=0, keepdims=True)
    projected = as_column(rhs_past) + jnp.sum(cross * coeff, axis=1, keepdims=True)
    inner = jnp.sum(inv_past * as_row(projected), axis=1, keepdims=True)
    coeff_ref[...] = coeff
    past_ref[...] = jnp.sum(inv_past * inner, axis=0, keepdims=True)


def solve_both(sums, n_cur):
    n_past = sums.shape[1] - n_cur
    shapes = (jax.ShapeDtypeStruct((1, n_cur), jnp.float32), jax.ShapeDtypeStruct((1, n_past), jnp.float32))
    coeff, past = pl.pallas_call(solve_kernel, out_shape=shapes)(sums)
    return coeff[0], past[0]


def body(
    fluid_press,
    iterate,
    displace,
    velocity,
    stiffness,
    owners,
    diff_cur,
    step_cur,
    diff_past,
    step_past,
):
    high = lax.Precision.HIGHEST
    tile_count = lax.axis_size("tile")
    line_count = displace.shape[0]
    slot_count = iterate.shape[0]
    per_pair = slot_count // tile_count
    n_cur = diff_cur.shape[0]
    owner_list = owners[:, 0]
    onehot = (owner_list[:, None] == jnp.arange(tile_count, dtype=jnp.int32)[None, :]).astype(
        jnp.float32
    )
    below = (jnp.arange(line_count)[:, None] > jnp.arange(line_count)[None, :]).astype(jnp.float32)
    earlier = jnp.dot(below, onehot, precision=high)
    rank_in = jnp.sum(earlier * onehot, axis=1).astype(jnp.int32)
    slot_of = owner_list * per_pair + rank_in
    chooser = (slot_of[:, None] == jnp.arange(slot_count, dtype=jnp.int32)[None, :]).astype(
        jnp.float32
    )
    counts = jnp.sum(onehot, axis=0)
    flags = (jnp.arange(per_pair, dtype=jnp.float32)[None, :] < counts[:, None]).astype(jnp.float32)
    lanes = fluid_press.shape[1]
    width = SUBSTEPS

    edge = jnp.concatenate([displace, velocity, stiffness], axis=1)
    edge_below, edge_above = halo_pair(edge, width, "tile")

    flag_rows = jnp.zeros((tile_count, 1, lanes), jnp.float32)
    flag_rows = flag_rows.at[:, 0, :per_pair].set(flags)
    sent = jnp.concatenate([fluid_press.reshape(tile_count, per_pair, lanes), flag_rows], axis=1)
    got = lax.all_to_all(sent, "tile", split_axis=0, concat_axis=0, tiled=True)
    returned = got[:, :per_pair, :].reshape(slot_count, lanes)
    mask = got[:, per_pair, :per_pair].reshape(slot_count)
    mask_half = mask.astype(jnp.bfloat16)

    cols = jnp.concatenate(
        [
            (diff_cur * mask_half[None, :, None]).reshape(n_cur, -1),
            (diff_past * mask_half[None, :, None]).reshape(diff_past.shape[0], -1),
        ],
        axis=0,
    )
    gram = lax.dot_general(cols, cols, (((1,), (1,)), ((), ())), preferred_element_type=jnp.float32)

    pressure = jnp.dot(chooser, returned, precision=high)
    press_below, press_above = halo_pair(pressure, width, "tile")
    def extended(middle, which):
        cut = slice(which * lanes, (which + 1) * lanes)
        return jnp.concatenate([edge_below[:, cut], middle, edge_above[:, cut]], axis=0)

    field = extended(displace, 0)
    speed = extended(velocity, 1)
    stiff = extended(stiffness, 2)
    press = jnp.concatenate([press_below, pressure, press_above], axis=0)
    for _ in range(SUBSTEPS):
        lapl = jnp.roll(field, 1, 0) + jnp.roll(field, -1, 0) + sides(field) - 4.0 * field
        speed = speed + step_dt * (stiff * lapl + press - damping * speed)
        field = field + step_dt * speed
    field = field[width : width + line_count]
    speed = speed[width : width + line_count]

    outgoing = jnp.dot(chooser.T, field, precision=high)
    x_tilde = lax.all_to_all(outgoing, "tile", split_axis=0, concat_axis=0, tiled=True)
    resid = to_half(mask[:, None] * (x_tilde - iterate))
    inner = jnp.concatenate(
        [
            jnp.sum(diff_cur.astype(jnp.float32) * resid[None], axis=(1, 2)),
            jnp.sum(diff_past.astype(jnp.float32) * resid[None], axis=(1, 2)),
        ]
    )
    summed = tree_sum(jnp.concatenate([gram, inner[None]], axis=0), "tile")
    coeff, past = solve_both(summed, n_cur)
    coeff_half = to_half(coeff)
    past_half = to_half(past)
    upd_cur = jnp.sum(coeff_half[:, None, None] * step_cur.astype(jnp.float32), axis=0)
    upd_past = jnp.sum(past_half[:, None, None] * step_past.astype(jnp.float32), axis=0)
    update = upd_cur - upd_past
    new_iterate = mask[:, None] * (x_tilde + update)
    return (new_iterate, field, speed)


def solution(mesh):
    placed = (
        P(("runs", "tile"), None),
        P(("runs", "tile"), None),
        P(("runs", "tile"), None),
        P(("runs", "tile"), None),
        P(("runs", "tile"), None),
        P(("runs", "tile"), None),
        P(None, ("runs", "tile"), None),
        P(None, ("runs", "tile"), None),
        P(None, ("runs", "tile"), None),
        P(None, ("runs", "tile"), None),
    )
    return jax.shard_map(
        body,
        mesh=mesh,
        in_specs=placed,
        out_specs=(P(("runs", "tile"), None), P(("runs", "tile"), None), P(("runs", "tile"), None)),
        check_vma=False,
    )
```

```python
import jax
import jax.numpy as jnp
from jax import lax
from jax.experimental import pallas as pl
from jax.sharding import PartitionSpec as P


SUBSTEPS = 4


step_dt = 1.0
damping = 0.05


def tree_parts(value, axis):
    count = lax.axis_size(axis)
    stride = 1
    while stride * 2 < count:
        value = value + lax.ppermute(value, axis, [(i, i ^ stride) for i in range(count)])
        stride *= 2
    return value, lax.ppermute(value, axis, [(i, i ^ stride) for i in range(count)])


def halo_pair(cells, width, axis):
    count = lax.axis_size(axis)
    below = lax.ppermute(cells[-width:], axis, [(i, (i + 1) % count) for i in range(count)])
    above = lax.ppermute(cells[:width], axis, [((i + 1) % count, i) for i in range(count)])
    return below, above


def to_half(value):
    return lax.reduce_precision(value, exponent_bits=8, mantissa_bits=7)


def sides(center):
    zero_col = jnp.zeros((center.shape[0], 1), jnp.float32)
    left = jnp.concatenate([zero_col, center[:, :-1]], 1)
    right = jnp.concatenate([center[:, 1:], zero_col], 1)
    return left + right


def eliminate(mats):
    state = []
    for a in mats:
        n = a.shape[0]
        rows = lax.broadcasted_iota(jnp.int32, (n, n), 0)
        cols = lax.broadcasted_iota(jnp.int32, (n, n), 1)
        state.append([a, jnp.where(rows == cols, 1.0, 0.0).astype(jnp.float32), rows, cols])
    for j in range(max(a.shape[0] for a in mats)):
        for item in state:
            a, m, rows, cols = item
            if j >= a.shape[0]:
                continue
            on_row = rows == j
            row = jnp.sum(jnp.where(on_row, a, 0.0), axis=0, keepdims=True)
            col = jnp.sum(jnp.where(cols == j, a, 0.0), axis=1, keepdims=True)
            pivot = jnp.sum(jnp.where(cols[:1] == j, row, 0.0), axis=1, keepdims=True)
            scale = 1.0 / jnp.sqrt(pivot)
            row = jnp.where(cols[:1] >= j, row * scale, 0.0)
            lower = jnp.where(rows[:, :1] > j, col * scale, 0.0)
            m_row = jnp.sum(jnp.where(on_row, m, 0.0), axis=0, keepdims=True) * scale
            item[0] = jnp.where(on_row, row, a - lower * row)
            item[1] = jnp.where(on_row, m_row, m - lower * m_row)
    return [item[1] for item in state]


def as_column(row):
    n = row.shape[1]
    eye = lax.broadcasted_iota(jnp.int32, (n, n), 0) == lax.broadcasted_iota(jnp.int32, (n, n), 1)
    return jnp.sum(jnp.where(eye, row, 0.0), axis=1, keepdims=True)


def as_row(col):
    n = col.shape[0]
    eye = lax.broadcasted_iota(jnp.int32, (n, n), 0) == lax.broadcasted_iota(jnp.int32, (n, n), 1)
    return jnp.sum(jnp.where(eye, col, 0.0), axis=0, keepdims=True)


def solve_kernel(own_ref, got_ref, coeff_ref, past_ref):
    n_cur = coeff_ref.shape[1]
    n_all = own_ref.shape[1]
    sums = own_ref[...] + got_ref[...]
    gram_cur = sums[:n_cur, :n_cur]
    gram_past = sums[n_cur:n_all, n_cur:n_all]
    cross = sums[n_cur:n_all, :n_cur]
    rhs_cur = sums[n_all:, :n_cur]
    rhs_past = sums[n_all:, n_cur:n_all]
    inv_cur, inv_past = eliminate([gram_cur, gram_past])
    inner = jnp.sum(inv_cur * rhs_cur, axis=1, keepdims=True)
    coeff = -jnp.sum(inv_cur * inner, axis=0, keepdims=True)
    projected = as_column(rhs_past) + jnp.sum(cross * coeff, axis=1, keepdims=True)
    inner = jnp.sum(inv_past * as_row(projected), axis=1, keepdims=True)
    coeff_ref[...] = coeff
    past_ref[...] = jnp.sum(inv_past * inner, axis=0, keepdims=True)


def solve_both(own, got, n_cur):
    n_past = own.shape[1] - n_cur
    shapes = (jax.ShapeDtypeStruct((1, n_cur), jnp.float32), jax.ShapeDtypeStruct((1, n_past), jnp.float32))
    coeff, past = pl.pallas_call(solve_kernel, out_shape=shapes)(own, got)
    return coeff[0], past[0]


def body(
    fluid_press,
    iterate,
    displace,
    velocity,
    stiffness,
    owners,
    diff_cur,
    step_cur,
    diff_past,
    step_past,
):
    high = lax.Precision.HIGHEST
    tile_count = lax.axis_size("tile")
    line_count = displace.shape[0]
    slot_count = iterate.shape[0]
    per_pair = slot_count // tile_count
    n_cur = diff_cur.shape[0]
    owner_list = owners[:, 0]
    onehot = (owner_list[:, None] == jnp.arange(tile_count, dtype=jnp.int32)[None, :]).astype(
        jnp.float32
    )
    below = (jnp.arange(line_count)[:, None] > jnp.arange(line_count)[None, :]).astype(jnp.float32)
    earlier = jnp.dot(below, onehot, precision=high)
    rank_in = jnp.sum(earlier * onehot, axis=1).astype(jnp.int32)
    slot_of = owner_list * per_pair + rank_in
    chooser = (slot_of[:, None] == jnp.arange(slot_count, dtype=jnp.int32)[None, :]).astype(
        jnp.float32
    )
    counts = jnp.sum(onehot, axis=0)
    flags = (jnp.arange(per_pair, dtype=jnp.float32)[None, :] < counts[:, None]).astype(jnp.float32)
    lanes = fluid_press.shape[1]
    width = SUBSTEPS

    edge = jnp.concatenate([displace, velocity, stiffness], axis=1)
    edge_below, edge_above = halo_pair(edge, width, "tile")

    flag_rows = jnp.zeros((tile_count, 1, lanes), jnp.float32)
    flag_rows = flag_rows.at[:, 0, :per_pair].set(flags)
    sent = jnp.concatenate([fluid_press.reshape(tile_count, per_pair, lanes), flag_rows], axis=1)
    got = lax.all_to_all(sent, "tile", split_axis=0, concat_axis=0, tiled=True)
    returned = got[:, :per_pair, :].reshape(slot_count, lanes)
    mask = got[:, per_pair, :per_pair].reshape(slot_count)
    mask_half = mask.astype(jnp.bfloat16)

    cols = jnp.concatenate(
        [
            (diff_cur * mask_half[None, :, None]).reshape(n_cur, -1),
            (diff_past * mask_half[None, :, None]).reshape(diff_past.shape[0], -1),
        ],
        axis=0,
    )
    gram = lax.dot_general(cols, cols, (((1,), (1,)), ((), ())), preferred_element_type=jnp.float32)

    pressure = jnp.dot(chooser, returned, precision=high)
    press_below, press_above = halo_pair(pressure, width, "tile")
    packed = jnp.concatenate(
        [
            jnp.concatenate([edge_below, press_below], axis=1),
            jnp.concatenate([edge, pressure], axis=1),
            jnp.concatenate([edge_above, press_above], axis=1),
        ],
        axis=0,
    )
    field = packed[:, :lanes]
    speed = packed[:, lanes : 2 * lanes]
    stiff = packed[:, 2 * lanes : 3 * lanes]
    press = packed[:, 3 * lanes :]
    for _ in range(SUBSTEPS):
        lapl = jnp.roll(field, 1, 0) + jnp.roll(field, -1, 0) + sides(field) - 4.0 * field
        speed = speed + step_dt * (stiff * lapl + press - damping * speed)
        field = field + step_dt * speed
    field = field[width : width + line_count]
    speed = speed[width : width + line_count]

    outgoing = jnp.dot(chooser.T, field, precision=high)
    x_tilde = lax.all_to_all(outgoing, "tile", split_axis=0, concat_axis=0, tiled=True)
    resid = to_half(mask[:, None] * (x_tilde - iterate))
    inner = jnp.concatenate(
        [
            jnp.sum(diff_cur.astype(jnp.float32) * resid[None], axis=(1, 2)),
            jnp.sum(diff_past.astype(jnp.float32) * resid[None], axis=(1, 2)),
        ]
    )
    own, got = tree_parts(jnp.concatenate([gram, inner[None]], axis=0), "tile")
    coeff, past = solve_both(own, got, n_cur)
    coeff_half = to_half(coeff)
    past_half = to_half(past)
    upd_cur = jnp.sum(coeff_half[:, None, None] * step_cur.astype(jnp.float32), axis=0)
    upd_past = jnp.sum(past_half[:, None, None] * step_past.astype(jnp.float32), axis=0)
    update = upd_cur - upd_past
    new_iterate = mask[:, None] * (x_tilde + update)
    return (new_iterate, field, speed)


def solution(mesh):
    placed = (
        P(("runs", "tile"), None),
        P(("runs", "tile"), None),
        P(("runs", "tile"), None),
        P(("runs", "tile"), None),
        P(("runs", "tile"), None),
        P(("runs", "tile"), None),
        P(None, ("runs", "tile"), None),
        P(None, ("runs", "tile"), None),
        P(None, ("runs", "tile"), None),
        P(None, ("runs", "tile"), None),
    )
    return jax.shard_map(
        body,
        mesh=mesh,
        in_specs=placed,
        out_specs=(P(("runs", "tile"), None), P(("runs", "tile"), None), P(("runs", "tile"), None)),
        check_vma=False,
    )
```
